32 devices in a mesh: blk: 8 (over y, x, core), slab: 4 (over z).
Axes of the slice: x: 2, y: 2, z: 4, core: 2. Of those that a mesh axis runs over, the one named last changes fastest.
Arguments:
- queries: bfloat16 [4096, 4096], P(('blk', 'slab')), may hold values from -8 to 8
- passages: bfloat16 [2816, 4096], P(('blk', 'slab')), may hold values from -6 to 6
- positive: int32 [4096], P(('blk', 'slab')), may hold values from 0 to 703
- hard_ids: int32 [4096, 8], P(('blk', 'slab')), may hold values from 0 to 2815, as said below
Outputs:
- query_loss: float32 [4096], P(('blk', 'slab'))
- query_grad: float32 [4096, 4096], P(('blk', 'slab'))
- passage_grad: float32 [2816, 4096], P(('blk', 'slab'))
The draws below stay inside these ranges and needn't reach their ends.
Inputs may be any that keep to these rules, and one draw needn't show every extreme that they name: `hard_ids`: passage row f * 88 + t lies on the device of flat index f = b * 4 + s. Of the hard-negative ids of the 128 queries of one device, at most 36 name rows that lie on any one device, and in every draw some device has exactly 36 ids on some one device.
All inputs are finite; a program needn't handle non-finite values.
Results may differ from the reference program's by a relative error of at most 0.008.
Values may be sent and summed in bfloat16 or wider, within the bound.
No kernel may reach another device: no remote copies, remote signals or barrier semaphores. Data moves between devices by JAX's collectives and lax.ppermute only.
A program may use at most 192 MiB of HBM per device.

```python
import math
import jax
import jax.numpy as jnp
from jax import lax

EMBED_WIDTH = 4096
HARD = 8
DEVICE_QUERIES = 128
PASSAGE_DEV = 88
SLOTS = 36
QUERIES = 4096
PASSAGES = 2816
SLAB_PASSAGES = 704
N_BLK = 8
N_SLAB = 4


def hard_table(key):
    base_key = jax.random.fold_in(key, 11)
    devices = N_BLK * N_SLAB
    slot_total = SLOTS * devices
    entries = DEVICE_QUERIES * HARD
    popular = jax.random.randint(jax.random.fold_in(base_key, 1), (devices,), 0, 4) == 0

    def one_device(device_key):
        key_perm, key_forced, key_order, key_local = jax.random.split(device_key, 4)
        shuffled = jax.random.permutation(key_perm, slot_total)
        forced = jax.random.randint(key_forced, (), 0, devices)
        owner_dev = shuffled // SLOTS
        grade = jnp.where(owner_dev == forced, 0, jnp.where(popular[owner_dev], 1, 2))
        ranking = grade * slot_total + jnp.arange(slot_total, dtype=jnp.int32)
        ordering = jnp.argsort(ranking)
        chosen = shuffled[ordering][:entries]
        chosen = jax.random.permutation(key_order, chosen)
        local_rows = jax.random.randint(key_local, (entries,), 0, PASSAGE_DEV)
        return chosen // SLOTS * PASSAGE_DEV + local_rows
    device_keys = jax.random.split(jax.random.fold_in(base_key, 2), devices)
    table_ids = jax.vmap(one_device)(device_keys)
    return table_ids.reshape(QUERIES, HARD).astype(jnp.int32)


def positive_table(key):
    return jax.random.randint(jax.random.fold_in(key, 41), (QUERIES,), 0, SLAB_PASSAGES).astype(jnp.int32)


def passage_table(key):
    base_key = jax.random.fold_in(key, 21)
    key_base, key_scale = jax.random.split(base_key, 2)
    base_rows = jnp.clip(jax.random.normal(key_base, (PASSAGES, EMBED_WIDTH), jnp.float32), -4.0, 4.0)
    row_scale = jnp.exp(jax.random.uniform(key_scale, (PASSAGES, 1), jnp.float32, math.log(0.7), math.log(1.4)))
    table_rows = base_rows * row_scale
    return (jnp.clip(table_rows, -6.0, 6.0), row_scale[:, 0])


def draw_passages(key, part):
    return passage_table(key)[0].astype(jnp.bfloat16)


def draw_hard_ids(key, part):
    return hard_table(key)


def draw_positive(key, part):
    return positive_table(key)


def draw_queries(key, part):
    table_rows, row_scale = passage_table(key)
    table_ids = hard_table(key)
    positive_pos = positive_table(key)
    base_key = jax.random.fold_in(key, 31)
    key_noise, key_near = jax.random.split(base_key, 2)
    query_index = jnp.arange(QUERIES, dtype=jnp.int32)
    slab_index = query_index // DEVICE_QUERIES % N_SLAB
    unit_factor = 1.0 / (3.0 * math.sqrt(EMBED_WIDTH))

    def pool_row(position):
        return (position // PASSAGE_DEV * N_SLAB + slab_index) * PASSAGE_DEV + position % PASSAGE_DEV

    def component(row_ids, logit_level):
        scale_sq = row_scale[row_ids] * row_scale[row_ids]
        return logit_level * unit_factor * table_rows[row_ids] / scale_sq[:, None]
    accum = component(pool_row(positive_pos), 11.6)
    near_count = 8
    near_pos = jax.random.randint(key_near, (QUERIES, near_count), 0, SLAB_PASSAGES).astype(jnp.int32)
    for column in range(near_count):
        accum = accum + component(pool_row(near_pos[:, column]), 6.0)
    for column in range(HARD):
        accum = accum + component(table_ids[:, column], 5.7)
    noise_rows = jnp.clip(jax.random.normal(key_noise, (QUERIES, EMBED_WIDTH), jnp.float32), -4.0, 4.0)
    result = accum + 0.05 * noise_rows
    return jnp.clip(result, -8.0, 8.0).astype(jnp.bfloat16)


def setup_inputs(seed: int = 0) -> dict:
    arg_keys = jax.random.split(jax.random.key(seed), 5)
    queries = draw_queries(jax.random.fold_in(arg_keys[4], 71), 0)
    passages = draw_passages(jax.random.fold_in(arg_keys[4], 71), 0)
    positive = draw_positive(jax.random.fold_in(arg_keys[4], 71), 0)
    hard_ids = draw_hard_ids(jax.random.fold_in(arg_keys[4], 71), 0)
    return {"queries": queries, "passages": passages, "positive": positive, "hard_ids": hard_ids}


def reference(queries, passages, positive, hard_ids):
    block_list = N_BLK
    slabs = N_SLAB
    devices = block_list * slabs
    logit_scale = 3.0 / math.sqrt(EMBED_WIDTH)

    def by_slab(array):
        per_rows = array.shape[0] // devices
        tail_dims = array.shape[1:]
        shaped = array.reshape((block_list, slabs, per_rows) + tail_dims)
        return jnp.swapaxes(shaped, 0, 1).reshape((slabs, block_list * per_rows) + tail_dims)

    def by_device(array):
        per_rows = array.shape[1] // block_list
        tail_dims = array.shape[2:]
        shaped = array.reshape((slabs, block_list, per_rows) + tail_dims)
        return jnp.swapaxes(shaped, 0, 1).reshape((devices * per_rows,) + tail_dims)
    slab_queries = by_slab(queries)
    slab_pool = by_slab(passages)
    slab_positive = by_slab(positive)
    pooled = jnp.einsum('sqd,sjd->sqj', slab_queries.astype(jnp.float32), slab_pool.astype(jnp.float32)) * logit_scale
    query_blocks = queries.reshape(devices, DEVICE_QUERIES, EMBED_WIDTH)
    id_blocks = hard_ids.reshape(devices, DEVICE_QUERIES, HARD)

    def hard_block(pair):
        block_query, block_ids = pair
        picked = passages[block_ids].astype(jnp.float32)
        return jnp.einsum('qd,qkd->qk', block_query.astype(jnp.float32), picked) * logit_scale
    hard_logits = lax.map(hard_block, (query_blocks, id_blocks)).reshape(QUERIES, HARD)
    slab_hard = by_slab(hard_logits)
    row_top = jnp.maximum(lax.optimization_barrier(jnp.max(pooled, axis=2)), lax.optimization_barrier(jnp.max(slab_hard, axis=2)))
    row_total = lax.optimization_barrier(jnp.sum(jnp.exp(pooled - row_top[..., None]), axis=2)) + lax.optimization_barrier(jnp.sum(jnp.exp(slab_hard - row_top[..., None]), axis=2))
    row_lse = row_top + jnp.log(row_total)
    onehot = (jnp.arange(SLAB_PASSAGES, dtype=jnp.int32)[None, None, :] == slab_positive[:, :, None]).astype(jnp.float32)
    query_loss = row_lse - lax.optimization_barrier(jnp.sum(onehot * pooled, axis=2))
    coef_pool = (jnp.exp(pooled - row_lse[..., None]) - onehot).astype(jnp.bfloat16)
    coef_hard = jnp.exp(slab_hard - row_lse[..., None]).astype(jnp.bfloat16)
    grad_pool = jnp.einsum('sqj,sjd->sqd', coef_pool.astype(jnp.float32), slab_pool.astype(jnp.float32))
    coef_global = by_device(coef_hard).reshape(devices, DEVICE_QUERIES, HARD)

    def hard_grad(triple):
        block_query, block_ids, block_coef = triple
        picked = passages[block_ids].astype(jnp.float32)
        return jnp.einsum('qk,qkd->qd', block_coef.astype(jnp.float32), picked)
    grad_hard = lax.map(hard_grad, (query_blocks, id_blocks, coef_global)).reshape(QUERIES, EMBED_WIDTH)
    query_grad = by_device(grad_pool) + grad_hard

    def slab_partial(pair):
        weight_factors, input_rows = pair
        running_partial = jnp.einsum('zsf,zsl->zfl', weight_factors.reshape(block_list, DEVICE_QUERIES, SLAB_PASSAGES).astype(jnp.float32), input_rows.reshape(block_list, DEVICE_QUERIES, EMBED_WIDTH).astype(jnp.float32))
        rounded = lax.optimization_barrier(running_partial.astype(jnp.bfloat16))
        return lax.optimization_barrier(jnp.sum(rounded.astype(jnp.float32), axis=0))
    pool_sum = lax.map(slab_partial, (coef_pool, slab_queries))
    passage_grad = by_device(pool_sum)

    def add_hard(carry, triple):
        block_query, block_ids, block_coef = triple
        terms = (block_coef.astype(jnp.float32)[:, :, None] * block_query.astype(jnp.float32)[:, None, :]).astype(jnp.bfloat16)
        terms = lax.optimization_barrier(terms).astype(jnp.float32)
        return (carry.at[block_ids.reshape(-1)].add(terms.reshape(-1, EMBED_WIDTH)), None)
    passage_grad = lax.scan(add_hard, passage_grad, (query_blocks, id_blocks, coef_global))[0]
    return (by_device(query_loss), query_grad, passage_grad)
```

```python
import math

import jax
import jax.numpy as jnp
from jax import lax
from jax.sharding import PartitionSpec as P


def per_device(queries, passages, positive, hard_ids):
    slabs = lax.axis_size("slab")
    my_slab = lax.axis_index("slab")
    query_rows_dev, model_width = queries.shape
    passage_rows_dev = passages.shape[0]
    hard_count = hard_ids.shape[1]
    logit_scale = 3.0 / math.sqrt(model_width)
    contract_rows = (((1,), (1,)), ((), ()))
    contract_cols = (((0,), (0,)), ((), ()))

    pool = lax.all_gather(passages, "blk", axis=0, tiled=True)
    pool_size = pool.shape[0]
    column_queries = lax.all_gather(queries, "slab", axis=0, tiled=True)
    column_ids = lax.all_gather(hard_ids, "slab", axis=0, tiled=True)
    column_rows = column_queries.shape[0]

    scores = (
        lax.dot_general(column_queries, pool, contract_rows, preferred_element_type=jnp.float32)
        * logit_scale
    )
    own_start = my_slab * query_rows_dev
    pooled = lax.dynamic_slice_in_dim(scores, own_start, query_rows_dev, axis=0)

    owner_dev = column_ids // passage_rows_dev
    owner_slab = owner_dev % slabs
    hard_pos = (owner_dev // slabs) * passage_rows_dev + column_ids % passage_rows_dev
    mine = owner_slab == my_slab
    hard_mine = jnp.where(mine, jnp.take_along_axis(scores, hard_pos, axis=1), 0.0)

    pool_max = jnp.max(pooled, axis=1)
    pool_sum = jnp.sum(jnp.exp(pooled - pool_max[:, None]), axis=1)
    payload = jnp.concatenate([hard_mine.reshape(-1), pool_max, pool_sum])
    gathered = lax.all_gather(payload, "slab", axis=0)
    hard_split = column_rows * hard_count
    hard_all = jnp.take_along_axis(
        gathered[:, :hard_split].reshape(slabs, column_rows, hard_count),
        owner_slab[None],
        axis=0,
    )[0]
    stats = gathered[:, hard_split:].reshape(slabs, 2, query_rows_dev)
    max_all = stats[:, 0].reshape(column_rows)
    sum_all = stats[:, 1].reshape(column_rows)

    row_top = jnp.maximum(max_all, jnp.max(hard_all, axis=1))
    row_total = sum_all * jnp.exp(max_all - row_top) + jnp.sum(
        jnp.exp(hard_all - row_top[:, None]), axis=1
    )
    lse_all = row_top + jnp.log(row_total)
    row_lse = lax.dynamic_slice_in_dim(lse_all, own_start, query_rows_dev)

    onehot = (jnp.arange(pool_size, dtype=jnp.int32)[None, :] == positive[:, None]).astype(
        jnp.float32
    )
    query_loss = row_lse - jnp.sum(onehot * pooled, axis=1)
    coef_pool = (jnp.exp(pooled - row_lse[:, None]) - onehot).astype(jnp.bfloat16)
    coef_hard = jnp.where(
        mine, jnp.exp(hard_mine - lse_all[:, None]).astype(jnp.bfloat16), jnp.zeros((), jnp.bfloat16)
    )
    hard_matrix = jnp.sum(
        jnp.where(
            hard_pos[:, :, None] == jnp.arange(pool_size, dtype=jnp.int32)[None, None, :],
            coef_hard.astype(jnp.float32)[:, :, None],
            0.0,
        ),
        axis=1,
    ).astype(jnp.bfloat16)

    hard_grad = jnp.dot(hard_matrix, pool, preferred_element_type=jnp.float32).astype(jnp.bfloat16)
    hard_grad = lax.psum_scatter(hard_grad, "slab", scatter_dimension=0, tiled=True)
    pool_grad = jnp.dot(coef_pool, pool, preferred_element_type=jnp.float32)
    query_grad = pool_grad + hard_grad.astype(jnp.float32)

    partial = lax.dot_general(
        coef_pool, queries, contract_cols, preferred_element_type=jnp.float32
    ) + lax.dot_general(hard_matrix, column_queries, contract_cols, preferred_element_type=jnp.float32)
    passage_grad = lax.psum_scatter(
        partial.astype(jnp.bfloat16), "blk", scatter_dimension=0, tiled=True
    ).astype(jnp.float32)
    return (query_loss, query_grad, passage_grad)


def solution(mesh):
    return jax.shard_map(
        per_device,
        mesh=mesh,
        in_specs=(
            P(("blk", "slab"), None),
            P(("blk", "slab"), None),
            P(("blk", "slab")),
            P(("blk", "slab"), None),
        ),
        out_specs=(P(("blk", "slab")), P(("blk", "slab"), None), P(("blk", "slab"), None)),
        check_vma=False,
    )
```

```python
import math

import jax
import jax.numpy as jnp
from jax import lax
from jax.sharding import PartitionSpec as P


def per_device(queries, passages, positive, hard_ids):
    slabs = lax.axis_size("slab")
    my_slab = lax.axis_index("slab")
    query_rows_dev, model_width = queries.shape
    passage_rows_dev = passages.shape[0]
    hard_count = hard_ids.shape[1]
    logit_scale = 3.0 / math.sqrt(model_width)
    contract_rows = (((1,), (1,)), ((), ()))
    contract_cols = (((0,), (0,)), ((), ()))

    pool = lax.all_gather(passages, "blk", axis=0, tiled=True)
    pool_size = pool.shape[0]
    column_queries = lax.all_to_all(
        jnp.broadcast_to(queries[None], (slabs,) + queries.shape), "slab", 0, 0, tiled=True
    ).reshape(slabs * query_rows_dev, model_width)
    column_ids = lax.all_gather(hard_ids, "slab", axis=0, tiled=True)
    column_rows = column_queries.shape[0]

    scores = (
        lax.dot_general(column_queries, pool, contract_rows, preferred_element_type=jnp.float32)
        * logit_scale
    )
    own_start = my_slab * query_rows_dev
    pooled = lax.dynamic_slice_in_dim(scores, own_start, query_rows_dev, axis=0)

    owner_dev = column_ids // passage_rows_dev
    owner_slab = owner_dev % slabs
    hard_pos = (owner_dev // slabs) * passage_rows_dev + column_ids % passage_rows_dev
    mine = owner_slab == my_slab
    pool_iota = jnp.arange(pool_size, dtype=jnp.int32)[None, None, :]
    hard_hit = (hard_pos[:, :, None] == pool_iota) & mine[:, :, None]
    hard_mine = jnp.sum(jnp.where(hard_hit, scores[:, None, :], 0.0), axis=2)

    pool_max = jnp.max(pooled, axis=1)
    pool_sum = jnp.sum(jnp.exp(pooled - pool_max[:, None]), axis=1)
    payload = jnp.concatenate([hard_mine.reshape(-1), pool_max, pool_sum])
    gathered = lax.all_gather(payload, "slab", axis=0)
    hard_split = column_rows * hard_count
    slab_iota = jnp.arange(slabs, dtype=jnp.int32)[:, None, None]
    hard_all = jnp.sum(
        jnp.where(
            owner_slab[None] == slab_iota,
            gathered[:, :hard_split].reshape(slabs, column_rows, hard_count),
            0.0,
        ),
        axis=0,
    )
    stats = gathered[:, hard_split:].reshape(slabs, 2, query_rows_dev)
    max_all = stats[:, 0].reshape(column_rows)
    sum_all = stats[:, 1].reshape(column_rows)

    row_top = jnp.maximum(max_all, jnp.max(hard_all, axis=1))
    row_total = sum_all * jnp.exp(max_all - row_top) + jnp.sum(
        jnp.exp(hard_all - row_top[:, None]), axis=1
    )
    lse_all = row_top + jnp.log(row_total)
    row_lse = lax.dynamic_slice_in_dim(lse_all, own_start, query_rows_dev)

    onehot = (jnp.arange(pool_size, dtype=jnp.int32)[None, :] == positive[:, None]).astype(
        jnp.float32
    )
    query_loss = row_lse - jnp.sum(onehot * pooled, axis=1)
    coef_pool = (jnp.exp(pooled - row_lse[:, None]) - onehot).astype(jnp.bfloat16)
    coef_hard = jnp.where(
        mine, jnp.exp(hard_mine - lse_all[:, None]).astype(jnp.bfloat16), jnp.zeros((), jnp.bfloat16)
    )
    hard_matrix = jnp.sum(
        jnp.where(hard_hit, coef_hard.astype(jnp.float32)[:, :, None], 0.0), axis=1
    ).astype(jnp.bfloat16)

    hard_grad = jnp.dot(hard_matrix, pool, preferred_element_type=jnp.float32).astype(jnp.bfloat16)
    hard_grad = lax.all_to_all(
        hard_grad.reshape(slabs, query_rows_dev, model_width), "slab", 0, 0, tiled=True
    )
    pool_grad = jnp.dot(coef_pool, pool, preferred_element_type=jnp.float32)
    query_grad = pool_grad + jnp.sum(hard_grad.astype(jnp.float32), axis=0)

    partial = lax.dot_general(
        coef_pool, queries, contract_cols, preferred_element_type=jnp.float32
    ) + lax.dot_general(hard_matrix, column_queries, contract_cols, preferred_element_type=jnp.float32)
    passage_grad = lax.psum_scatter(
        partial.astype(jnp.bfloat16), "blk", scatter_dimension=0, tiled=True
    ).astype(jnp.float32)
    return (query_loss, query_grad, passage_grad)


def solution(mesh):
    return jax.shard_map(
        per_device,
        mesh=mesh,
        in_specs=(
            P(("blk", "slab"), None),
            P(("blk", "slab"), None),
            P(("blk", "slab")),
            P(("blk", "slab"), None),
        ),
        out_specs=(P(("blk", "slab")), P(("blk", "slab"), None), P(("blk", "slab"), None)),
        check_vma=False,
    )
```

```python
import math

import jax
import jax.numpy as jnp
from jax import lax
from jax.sharding import PartitionSpec as P


def per_device(queries, passages, positive, hard_ids):
    slabs = lax.axis_size("slab")
    my_slab = lax.axis_index("slab")
    query_rows_dev, model_width = queries.shape
    passage_rows_dev = passages.shape[0]
    hard_count = hard_ids.shape[1]
    logit_scale = 3.0 / math.sqrt(model_width)
    contract_rows = (((1,), (1,)), ((), ()))
    contract_cols = (((0,), (0,)), ((), ()))

    pool = lax.all_gather(passages, "blk", axis=0, tiled=True)
    pool_size = pool.shape[0]
    ring_down = [(i, (i - 1) % slabs) for i in range(slabs)]
    query_blocks = [queries]
    id_blocks = [hard_ids]
    for _ in range(slabs - 1):
        query_blocks.append(lax.ppermute(query_blocks[-1], "slab", ring_down))
        id_blocks.append(lax.ppermute(id_blocks[-1], "slab", ring_down))

    def to_origin(blocks):
        doubled = jnp.concatenate(blocks + blocks, axis=0)
        start = ((slabs - my_slab) % slabs) * blocks[0].shape[0]
        return lax.dynamic_slice_in_dim(doubled, start, slabs * blocks[0].shape[0], axis=0)

    column_queries = to_origin(query_blocks)
    column_ids = to_origin(id_blocks)
    column_rows = column_queries.shape[0]

    scores = (
        lax.dot_general(column_queries, pool, contract_rows, preferred_element_type=jnp.float32)
        * logit_scale
    )
    own_start = my_slab * query_rows_dev
    pooled = lax.dynamic_slice_in_dim(scores, own_start, query_rows_dev, axis=0)

    owner_dev = column_ids // passage_rows_dev
    owner_slab = owner_dev % slabs
    hard_pos = (owner_dev // slabs) * passage_rows_dev + column_ids % passage_rows_dev
    mine = owner_slab == my_slab
    pool_iota = jnp.arange(pool_size, dtype=jnp.int32)[None, None, :]
    hard_hit = (hard_pos[:, :, None] == pool_iota) & mine[:, :, None]
    hard_mine = jnp.sum(jnp.where(hard_hit, scores[:, None, :], 0.0), axis=2)

    pool_max = jnp.max(pooled, axis=1)
    pool_sum = jnp.sum(jnp.exp(pooled - pool_max[:, None]), axis=1)
    payload = jnp.concatenate([hard_mine.reshape(-1), pool_max, pool_sum])
    gathered = lax.all_gather(payload, "slab", axis=0)
    hard_split = column_rows * hard_count
    slab_iota = jnp.arange(slabs, dtype=jnp.int32)[:, None, None]
    hard_all = jnp.sum(
        jnp.where(
            owner_slab[None] == slab_iota,
            gathered[:, :hard_split].reshape(slabs, column_rows, hard_count),
            0.0,
        ),
        axis=0,
    )
    stats = gathered[:, hard_split:].reshape(slabs, 2, query_rows_dev)
    max_all = stats[:, 0].reshape(column_rows)
    sum_all = stats[:, 1].reshape(column_rows)

    row_top = jnp.maximum(max_all, jnp.max(hard_all, axis=1))
    row_total = sum_all * jnp.exp(max_all - row_top) + jnp.sum(
        jnp.exp(hard_all - row_top[:, None]), axis=1
    )
    lse_all = row_top + jnp.log(row_total)
    row_lse = lax.dynamic_slice_in_dim(lse_all, own_start, query_rows_dev)

    onehot = (jnp.arange(pool_size, dtype=jnp.int32)[None, :] == positive[:, None]).astype(
        jnp.float32
    )
    query_loss = row_lse - jnp.sum(onehot * pooled, axis=1)
    coef_pool = (jnp.exp(pooled - row_lse[:, None]) - onehot).astype(jnp.bfloat16)
    coef_hard = jnp.where(
        mine, jnp.exp(hard_mine - lse_all[:, None]).astype(jnp.bfloat16), jnp.zeros((), jnp.bfloat16)
    )
    hard_matrix = jnp.sum(
        jnp.where(hard_hit, coef_hard.astype(jnp.float32)[:, :, None], 0.0), axis=1
    ).astype(jnp.bfloat16)

    hard_grad = jnp.dot(hard_matrix, pool, preferred_element_type=jnp.float32).reshape(
        slabs, query_rows_dev, model_width
    )

    def grad_for(offset):
        return lax.dynamic_index_in_dim(hard_grad, (my_slab + offset) % slabs, keepdims=False)

    carried = grad_for(1)
    for step in range(1, slabs):
        carried = lax.ppermute(carried.astype(jnp.bfloat16), "slab", ring_down).astype(jnp.float32)
        carried = carried + grad_for((step + 1) % slabs)
    pool_grad = jnp.dot(coef_pool, pool, preferred_element_type=jnp.float32)
    query_grad = pool_grad + carried

    partial = lax.dot_general(
        coef_pool, queries, contract_cols, preferred_element_type=jnp.float32
    ) + lax.dot_general(hard_matrix, column_queries, contract_cols, preferred_element_type=jnp.float32)
    passage_grad = lax.psum_scatter(
        partial.astype(jnp.bfloat16), "blk", scatter_dimension=0, tiled=True
    ).astype(jnp.float32)
    return (query_loss, query_grad, passage_grad)


def solution(mesh):
    return jax.shard_map(
        per_device,
        mesh=mesh,
        in_specs=(
            P(("blk", "slab"), None),
            P(("blk", "slab"), None),
            P(("blk", "slab")),
            P(("blk", "slab"), None),
        ),
        out_specs=(P(("blk", "slab")), P(("blk", "slab"), None), P(("blk", "slab"), None)),
        check_vma=False,
    )
```

```python
import math

import jax
import jax.numpy as jnp
from jax import lax
from jax.sharding import PartitionSpec as P


def per_device(queries, passages, positive, hard_ids):
    slabs = lax.axis_size("slab")
    my_slab = lax.axis_index("slab")
    query_rows_dev, model_width = queries.shape
    passage_rows_dev = passages.shape[0]
    hard_count = hard_ids.shape[1]
    logit_scale = 3.0 / math.sqrt(model_width)
    contract_rows = (((1,), (1,)), ((), ()))
    contract_cols = (((0,), (0,)), ((), ()))

    pool = lax.all_gather(passages, "blk", axis=0, tiled=True)
    pool_size = pool.shape[0]

    ring_down = [(i, (i - 1) % slabs) for i in range(slabs)]
    query_blocks = [queries]
    id_blocks = [hard_ids]
    for _ in range(slabs - 1):
        query_blocks.append(lax.ppermute(query_blocks[-1], "slab", ring_down))
        id_blocks.append(lax.ppermute(id_blocks[-1], "slab", ring_down))

    def to_origin(x):
        doubled = jnp.concatenate([x, x], axis=0)
        return lax.dynamic_slice_in_dim(doubled, (slabs - my_slab) % slabs, slabs, axis=0)

    def to_ring(x):
        doubled = jnp.concatenate([x, x], axis=0)
        return lax.dynamic_slice_in_dim(doubled, my_slab, slabs, axis=0)

    scores = jnp.concatenate(
        [
            lax.dot_general(block, pool, contract_rows, preferred_element_type=jnp.float32)
            for block in query_blocks
        ],
        axis=0,
    ) * logit_scale
    column_ids = jnp.concatenate(id_blocks, axis=0)
    column_rows = column_ids.shape[0]
    pooled = scores[:query_rows_dev]

    owner_dev = column_ids // passage_rows_dev
    owner_slab = owner_dev % slabs
    hard_pos = (owner_dev // slabs) * passage_rows_dev + column_ids % passage_rows_dev
    mine = owner_slab == my_slab
    pool_iota = jnp.arange(pool_size, dtype=jnp.int32)[None, None, :]
    hard_hit = (hard_pos[:, :, None] == pool_iota) & mine[:, :, None]
    hard_mine = jnp.sum(jnp.where(hard_hit, scores[:, None, :], 0.0), axis=2)

    pool_max = jnp.max(pooled, axis=1)
    pool_sum = jnp.sum(jnp.exp(pooled - pool_max[:, None]), axis=1)
    hard_origin = to_origin(hard_mine.reshape(slabs, query_rows_dev * hard_count))
    payload = jnp.concatenate([hard_origin.reshape(-1), pool_max, pool_sum])
    gathered = lax.all_gather(payload, "slab", axis=0)
    hard_split = column_rows * hard_count
    owner_origin = to_origin(owner_slab.reshape(slabs, query_rows_dev * hard_count))
    slab_iota = jnp.arange(slabs, dtype=jnp.int32)[:, None, None]
    hard_all = jnp.sum(
        jnp.where(
            owner_origin[None] == slab_iota,
            gathered[:, :hard_split].reshape(slabs, slabs, query_rows_dev * hard_count),
            0.0,
        ),
        axis=0,
    )
    hard_all = to_ring(hard_all).reshape(column_rows, hard_count)
    stats = to_ring(gathered[:, hard_split:].reshape(slabs, 2, query_rows_dev))
    max_all = stats[:, 0].reshape(column_rows)
    sum_all = stats[:, 1].reshape(column_rows)

    row_top = jnp.maximum(max_all, jnp.max(hard_all, axis=1))
    row_total = sum_all * jnp.exp(max_all - row_top) + jnp.sum(
        jnp.exp(hard_all - row_top[:, None]), axis=1
    )
    lse_all = row_top + jnp.log(row_total)
    row_lse = lse_all[:query_rows_dev]

    onehot = (jnp.arange(pool_size, dtype=jnp.int32)[None, :] == positive[:, None]).astype(
        jnp.float32
    )
    query_loss = row_lse - jnp.sum(onehot * pooled, axis=1)
    coef_pool = (jnp.exp(pooled - row_lse[:, None]) - onehot).astype(jnp.bfloat16)
    coef_hard = jnp.where(
        mine, jnp.exp(hard_mine - lse_all[:, None]).astype(jnp.bfloat16), jnp.zeros((), jnp.bfloat16)
    )
    hard_matrix = jnp.sum(
        jnp.where(hard_hit, coef_hard.astype(jnp.float32)[:, :, None], 0.0), axis=1
    ).astype(jnp.bfloat16)

    def grad_for(block):
        rows = hard_matrix[block * query_rows_dev : (block + 1) * query_rows_dev]
        return jnp.dot(rows, pool, preferred_element_type=jnp.float32)

    carried = grad_for(1)
    for step in range(1, slabs):
        carried = lax.ppermute(carried.astype(jnp.bfloat16), "slab", ring_down).astype(jnp.float32)
        carried = carried + grad_for((step + 1) % slabs)
    pool_grad = jnp.dot(coef_pool, pool, preferred_element_type=jnp.float32)
    query_grad = pool_grad + carried

    column_queries = jnp.concatenate(query_blocks, axis=0)
    partial = lax.dot_general(
        coef_pool, queries, contract_cols, preferred_element_type=jnp.float32
    ) + lax.dot_general(hard_matrix, column_queries, contract_cols, preferred_element_type=jnp.float32)
    passage_grad = lax.psum_scatter(
        partial.astype(jnp.bfloat16), "blk", scatter_dimension=0, tiled=True
    ).astype(jnp.float32)
    return (query_loss, query_grad, passage_grad)


def solution(mesh):
    return jax.shard_map(
        per_device,
        mesh=mesh,
        in_specs=(
            P(("blk", "slab"), None),
            P(("blk", "slab"), None),
            P(("blk", "slab")),
            P(("blk", "slab"), None),
        ),
        out_specs=(P(("blk", "slab")), P(("blk", "slab"), None), P(("blk", "slab"), None)),
        check_vma=False,
    )
```

```python
import math

import jax
import jax.numpy as jnp
from jax import lax
from jax.sharding import PartitionSpec as P


def per_device(queries, passages, positive, hard_ids):
    slabs = lax.axis_size("slab")
    my_slab = lax.axis_index("slab")
    query_rows_dev, model_width = queries.shape
    passage_rows_dev = passages.shape[0]
    hard_count = hard_ids.shape[1]
    logit_scale = 3.0 / math.sqrt(model_width)
    contract_rows = (((1,), (1,)), ((), ()))
    contract_cols = (((0,), (0,)), ((), ()))

    pool = lax.all_gather(passages, "blk", axis=0, tiled=True)
    pool_size = pool.shape[0]

    ring_down = [(i, (i - 1) % slabs) for i in range(slabs)]
    chunks = 2
    chunk_rows = query_rows_dev // chunks

    def ring_gather(x):
        parts = [x[c * chunk_rows : (c + 1) * chunk_rows] for c in range(chunks)]
        blocks = [x]
        for _ in range(slabs - 1):
            parts = [lax.ppermute(part, "slab", ring_down) for part in parts]
            blocks.append(jnp.concatenate(parts, axis=0))
        return blocks

    query_blocks = ring_gather(queries)
    id_blocks = ring_gather(hard_ids)

    def to_origin(x):
        doubled = jnp.concatenate([x, x], axis=0)
        return lax.dynamic_slice_in_dim(doubled, (slabs - my_slab) % slabs, slabs, axis=0)

    def to_ring(x):
        doubled = jnp.concatenate([x, x], axis=0)
        return lax.dynamic_slice_in_dim(doubled, my_slab, slabs, axis=0)

    scores = jnp.concatenate(
        [
            lax.dot_general(block, pool, contract_rows, preferred_element_type=jnp.float32)
            for block in query_blocks
        ],
        axis=0,
    ) * logit_scale
    column_ids = jnp.concatenate(id_blocks, axis=0)
    column_rows = column_ids.shape[0]
    pooled = scores[:query_rows_dev]

    owner_dev = column_ids // passage_rows_dev
    owner_slab = owner_dev % slabs
    hard_pos = (owner_dev // slabs) * passage_rows_dev + column_ids % passage_rows_dev
    mine = owner_slab == my_slab
    pool_iota = jnp.arange(pool_size, dtype=jnp.int32)[None, None, :]
    hard_hit = (hard_pos[:, :, None] == pool_iota) & mine[:, :, None]
    hard_mine = jnp.sum(jnp.where(hard_hit, scores[:, None, :], 0.0), axis=2)

    pool_max = jnp.max(pooled, axis=1)
    pool_sum = jnp.sum(jnp.exp(pooled - pool_max[:, None]), axis=1)
    hard_origin = to_origin(hard_mine.reshape(slabs, query_rows_dev * hard_count))
    payload = jnp.concatenate([hard_origin.reshape(-1), pool_max, pool_sum])
    gathered = lax.all_gather(payload, "slab", axis=0)
    hard_split = column_rows * hard_count
    owner_origin = to_origin(owner_slab.reshape(slabs, query_rows_dev * hard_count))
    slab_iota = jnp.arange(slabs, dtype=jnp.int32)[:, None, None]
    hard_all = jnp.sum(
        jnp.where(
            owner_origin[None] == slab_iota,
            gathered[:, :hard_split].reshape(slabs, slabs, query_rows_dev * hard_count),
            0.0,
        ),
        axis=0,
    )
    hard_all = to_ring(hard_all).reshape(column_rows, hard_count)
    stats = to_ring(gathered[:, hard_split:].reshape(slabs, 2, query_rows_dev))
    max_all = stats[:, 0].reshape(column_rows)
    sum_all = stats[:, 1].reshape(column_rows)

    row_top = jnp.maximum(max_all, jnp.max(hard_all, axis=1))
    row_total = sum_all * jnp.exp(max_all - row_top) + jnp.sum(
        jnp.exp(hard_all - row_top[:, None]), axis=1
    )
    lse_all = row_top + jnp.log(row_total)
    row_lse = lse_all[:query_rows_dev]

    onehot = (jnp.arange(pool_size, dtype=jnp.int32)[None, :] == positive[:, None]).astype(
        jnp.float32
    )
    query_loss = row_lse - jnp.sum(onehot * pooled, axis=1)
    coef_pool = (jnp.exp(pooled - row_lse[:, None]) - onehot).astype(jnp.bfloat16)
    coef_hard = jnp.where(
        mine, jnp.exp(hard_mine - lse_all[:, None]).astype(jnp.bfloat16), jnp.zeros((), jnp.bfloat16)
    )
    hard_matrix = jnp.sum(
        jnp.where(hard_hit, coef_hard.astype(jnp.float32)[:, :, None], 0.0), axis=1
    ).astype(jnp.bfloat16)

    def grad_for(block):
        rows = hard_matrix[block * query_rows_dev : (block + 1) * query_rows_dev]
        return jnp.dot(rows, pool, preferred_element_type=jnp.float32)

    def chunk_of(x, c):
        return x[c * chunk_rows : (c + 1) * chunk_rows]

    carried = [chunk_of(grad_for(1), c) for c in range(chunks)]
    for step in range(1, slabs):
        nxt = grad_for((step + 1) % slabs)
        carried = [
            lax.ppermute(part.astype(jnp.bfloat16), "slab", ring_down).astype(jnp.float32)
            + chunk_of(nxt, c)
            for c, part in enumerate(carried)
        ]
    carried = jnp.concatenate(carried, axis=0)
    pool_grad = jnp.dot(coef_pool, pool, preferred_element_type=jnp.float32)
    query_grad = pool_grad + carried

    column_queries = jnp.concatenate(query_blocks, axis=0)
    partial = lax.dot_general(
        coef_pool, queries, contract_cols, preferred_element_type=jnp.float32
    ) + lax.dot_general(hard_matrix, column_queries, contract_cols, preferred_element_type=jnp.float32)
    passage_grad = lax.psum_scatter(
        partial.astype(jnp.bfloat16), "blk", scatter_dimension=0, tiled=True
    ).astype(jnp.float32)
    return (query_loss, query_grad, passage_grad)


def solution(mesh):
    return jax.shard_map(
        per_device,
        mesh=mesh,
        in_specs=(
            P(("blk", "slab"), None),
            P(("blk", "slab"), None),
            P(("blk", "slab")),
            P(("blk", "slab"), None),
        ),
        out_specs=(P(("blk", "slab")), P(("blk", "slab"), None), P(("blk", "slab"), None)),
        check_vma=False,
    )
```

```python
import math

import jax
import jax.numpy as jnp
from jax import lax
from jax.sharding import PartitionSpec as P


def per_device(queries, passages, positive, hard_ids):
    slabs = lax.axis_size("slab")
    my_slab = lax.axis_index("slab")
    query_rows_dev, model_width = queries.shape
    passage_rows_dev = passages.shape[0]
    hard_count = hard_ids.shape[1]
    logit_scale = 3.0 / math.sqrt(model_width)
    contract_rows = (((1,), (1,)), ((), ()))
    contract_cols = (((0,), (0,)), ((), ()))

    pool = lax.all_gather(passages, "blk", axis=0, tiled=True)
    pool_size = pool.shape[0]

    ring_down = [(i, (i - 1) % slabs) for i in range(slabs)]
    ring_up = [(i, (i + 1) % slabs) for i in range(slabs)]
    steps_down = slabs // 2
    steps_up = slabs - 1 - steps_down

    def ring_gather(x):
        blocks = [x] * slabs
        current = x
        for step in range(1, steps_down + 1):
            current = lax.ppermute(current, "slab", ring_down)
            blocks[step] = current
        current = x
        for step in range(1, steps_up + 1):
            current = lax.ppermute(current, "slab", ring_up)
            blocks[slabs - step] = current
        return blocks

    query_blocks = ring_gather(queries)
    id_blocks = ring_gather(hard_ids)

    def to_origin(x):
        doubled = jnp.concatenate([x, x], axis=0)
        return lax.dynamic_slice_in_dim(doubled, (slabs - my_slab) % slabs, slabs, axis=0)

    def to_ring(x):
        doubled = jnp.concatenate([x, x], axis=0)
        return lax.dynamic_slice_in_dim(doubled, my_slab, slabs, axis=0)

    scores = jnp.concatenate(
        [
            lax.dot_general(block, pool, contract_rows, preferred_element_type=jnp.float32)
            for block in query_blocks
        ],
        axis=0,
    ) * logit_scale
    column_ids = jnp.concatenate(id_blocks, axis=0)
    column_rows = column_ids.shape[0]
    pooled = scores[:query_rows_dev]

    owner_dev = column_ids // passage_rows_dev
    owner_slab = owner_dev % slabs
    hard_pos = (owner_dev // slabs) * passage_rows_dev + column_ids % passage_rows_dev
    mine = owner_slab == my_slab
    pool_iota = jnp.arange(pool_size, dtype=jnp.int32)[None, None, :]
    hard_hit = (hard_pos[:, :, None] == pool_iota) & mine[:, :, None]
    hard_mine = jnp.sum(jnp.where(hard_hit, scores[:, None, :], 0.0), axis=2)

    pool_max = jnp.max(pooled, axis=1)
    pool_sum = jnp.sum(jnp.exp(pooled - pool_max[:, None]), axis=1)
    hard_origin = to_origin(hard_mine.reshape(slabs, query_rows_dev * hard_count))
    payload = jnp.concatenate([hard_origin.reshape(-1), pool_max, pool_sum])
    gathered = to_origin(
        jnp.stack(
            [payload]
            + [
                lax.ppermute(payload, "slab", [(i, (i - t) % slabs) for i in range(slabs)])
                for t in range(1, slabs)
            ]
        )
    )
    hard_split = column_rows * hard_count
    owner_origin = to_origin(owner_slab.reshape(slabs, query_rows_dev * hard_count))
    slab_iota = jnp.arange(slabs, dtype=jnp.int32)[:, None, None]
    hard_all = jnp.sum(
        jnp.where(
            owner_origin[None] == slab_iota,
            gathered[:, :hard_split].reshape(slabs, slabs, query_rows_dev * hard_count),
            0.0,
        ),
        axis=0,
    )
    hard_all = to_ring(hard_all).reshape(column_rows, hard_count)
    stats = to_ring(gathered[:, hard_split:].reshape(slabs, 2, query_rows_dev))
    max_all = stats[:, 0].reshape(column_rows)
    sum_all = stats[:, 1].reshape(column_rows)

    row_top = jnp.maximum(max_all, jnp.max(hard_all, axis=1))
    row_total = sum_all * jnp.exp(max_all - row_top) + jnp.sum(
        jnp.exp(hard_all - row_top[:, None]), axis=1
    )
    lse_all = row_top + jnp.log(row_total)
    row_lse = lse_all[:query_rows_dev]

    onehot = (jnp.arange(pool_size, dtype=jnp.int32)[None, :] == positive[:, None]).astype(
        jnp.float32
    )
    query_loss = row_lse - jnp.sum(onehot * pooled, axis=1)
    coef_pool = (jnp.exp(pooled - row_lse[:, None]) - onehot).astype(jnp.bfloat16)
    coef_hard = jnp.where(
        mine, jnp.exp(hard_mine - lse_all[:, None]).astype(jnp.bfloat16), jnp.zeros((), jnp.bfloat16)
    )
    hard_matrix = jnp.sum(
        jnp.where(hard_hit, coef_hard.astype(jnp.float32)[:, :, None], 0.0), axis=1
    ).astype(jnp.bfloat16)

    def grad_for(block):
        rows = hard_matrix[block * query_rows_dev : (block + 1) * query_rows_dev]
        return jnp.dot(rows, pool, preferred_element_type=jnp.float32)

    def hop(part, perm):
        return lax.ppermute(part.astype(jnp.bfloat16), "slab", perm).astype(jnp.float32)

    carried = grad_for(0)
    if steps_down:
        down = grad_for(slabs - steps_down)
        for step in range(1, steps_down):
            down = hop(down, ring_down) + grad_for(slabs - steps_down + step)
        carried = carried + hop(down, ring_down)
    if steps_up:
        up = grad_for(steps_up)
        for step in range(1, steps_up):
            up = hop(up, ring_up) + grad_for(steps_up - step)
        carried = carried + hop(up, ring_up)
    pool_grad = jnp.dot(coef_pool, pool, preferred_element_type=jnp.float32)
    query_grad = pool_grad + carried

    column_queries = jnp.concatenate(query_blocks, axis=0)
    partial = lax.dot_general(
        coef_pool, queries, contract_cols, preferred_element_type=jnp.float32
    ) + lax.dot_general(hard_matrix, column_queries, contract_cols, preferred_element_type=jnp.float32)
    passage_grad = lax.psum_scatter(
        partial.astype(jnp.bfloat16), "blk", scatter_dimension=0, tiled=True
    ).astype(jnp.float32)
    return (query_loss, query_grad, passage_grad)


def solution(mesh):
    return jax.shard_map(
        per_device,
        mesh=mesh,
        in_specs=(
            P(("blk", "slab"), None),
            P(("blk", "slab"), None),
            P(("blk", "slab")),
            P(("blk", "slab"), None),
        ),
        out_specs=(P(("blk", "slab")), P(("blk", "slab"), None), P(("blk", "slab"), None)),
        check_vma=False,
    )
```

```python
import math

import jax
import jax.numpy as jnp
from jax import lax
from jax.sharding import PartitionSpec as P


def per_device(queries, passages, positive, hard_ids):
    slabs = lax.axis_size("slab")
    my_slab = lax.axis_index("slab")
    query_rows_dev, model_width = queries.shape
    passage_rows_dev = passages.shape[0]
    hard_count = hard_ids.shape[1]
    logit_scale = 3.0 / math.sqrt(model_width)
    contract_rows = (((1,), (1,)), ((), ()))
    contract_cols = (((0,), (0,)), ((), ()))

    pool = lax.all_gather(passages, "blk", axis=0, tiled=True)
    pool_size = pool.shape[0]

    ring_down = [(i, (i - 1) % slabs) for i in range(slabs)]
    ring_up = [(i, (i + 1) % slabs) for i in range(slabs)]
    steps_down = slabs // 2
    steps_up = slabs - 1 - steps_down

    def ring_gather(x):
        blocks = [x] * slabs
        current = x
        for step in range(1, steps_down + 1):
            current = lax.ppermute(current, "slab", ring_down)
            blocks[step] = current
        current = x
        for step in range(1, steps_up + 1):
            current = lax.ppermute(current, "slab", ring_up)
            blocks[slabs - step] = current
        return blocks

    query_blocks = ring_gather(queries)
    id_blocks = ring_gather(hard_ids)

    def to_origin(x):
        doubled = jnp.concatenate([x, x], axis=0)
        return lax.dynamic_slice_in_dim(doubled, (slabs - my_slab) % slabs, slabs, axis=0)

    def to_ring(x):
        doubled = jnp.concatenate([x, x], axis=0)
        return lax.dynamic_slice_in_dim(doubled, my_slab, slabs, axis=0)

    scores = jnp.concatenate(
        [
            lax.dot_general(block, pool, contract_rows, preferred_element_type=jnp.float32)
            for block in query_blocks
        ],
        axis=0,
    ) * logit_scale
    column_ids = jnp.concatenate(id_blocks, axis=0)
    column_rows = column_ids.shape[0]
    pooled = scores[:query_rows_dev]

    owner_dev = column_ids // passage_rows_dev
    owner_slab = owner_dev % slabs
    hard_pos = (owner_dev // slabs) * passage_rows_dev + column_ids % passage_rows_dev
    mine = owner_slab == my_slab
    pool_iota = jnp.arange(pool_size, dtype=jnp.int32)[None, None, :]
    hard_hit = (hard_pos[:, :, None] == pool_iota) & mine[:, :, None]
    hard_mine = jnp.sum(jnp.where(hard_hit, scores[:, None, :], 0.0), axis=2)

    pool_max = jnp.max(pooled, axis=1)
    pool_sum = jnp.sum(jnp.exp(pooled - pool_max[:, None]), axis=1)
    hard_origin = to_origin(hard_mine.reshape(slabs, query_rows_dev * hard_count))
    payload = jnp.concatenate([hard_origin.reshape(-1), pool_max, pool_sum])
    gathered = to_origin(
        jnp.stack(
            [payload]
            + [
                lax.ppermute(payload, "slab", [(i, (i - t) % slabs) for i in range(slabs)])
                for t in range(1, slabs)
            ]
        )
    )
    hard_split = column_rows * hard_count
    owner_origin = to_origin(owner_slab.reshape(slabs, query_rows_dev * hard_count))
    slab_iota = jnp.arange(slabs, dtype=jnp.int32)[:, None, None]
    hard_all = jnp.sum(
        jnp.where(
            owner_origin[None] == slab_iota,
            gathered[:, :hard_split].reshape(slabs, slabs, query_rows_dev * hard_count),
            0.0,
        ),
        axis=0,
    )
    hard_all = to_ring(hard_all).reshape(column_rows, hard_count)
    stats = to_ring(gathered[:, hard_split:].reshape(slabs, 2, query_rows_dev))
    max_all = stats[:, 0].reshape(column_rows)
    sum_all = stats[:, 1].reshape(column_rows)

    row_top = jnp.maximum(max_all, jnp.max(hard_all, axis=1))
    row_total = sum_all * jnp.exp(max_all - row_top) + jnp.sum(
        jnp.exp(hard_all - row_top[:, None]), axis=1
    )
    lse_all = row_top + jnp.log(row_total)
    row_lse = lse_all[:query_rows_dev]

    onehot = (jnp.arange(pool_size, dtype=jnp.int32)[None, :] == positive[:, None]).astype(
        jnp.float32
    )
    query_loss = row_lse - jnp.sum(onehot * pooled, axis=1)
    coef_pool = (jnp.exp(pooled - row_lse[:, None]) - onehot).astype(jnp.bfloat16)
    coef_hard = jnp.where(
        mine, jnp.exp(hard_mine - lse_all[:, None]).astype(jnp.bfloat16), jnp.zeros((), jnp.bfloat16)
    )
    hard_matrix = jnp.sum(
        jnp.where(hard_hit, coef_hard.astype(jnp.float32)[:, :, None], 0.0), axis=1
    ).astype(jnp.bfloat16)

    far_below = -1e30
    local_max = jnp.max(jnp.where(mine, hard_mine, far_below), axis=1)
    local_weight = jnp.where(mine, jnp.exp(hard_mine - local_max[:, None]), 0.0)
    weight_matrix = jnp.sum(
        jnp.where(hard_hit, local_weight.astype(jnp.bfloat16).astype(jnp.float32)[:, :, None], 0.0),
        axis=1,
    ).astype(jnp.bfloat16)

    def rows_of(x, block):
        return x[block * query_rows_dev : (block + 1) * query_rows_dev]

    def scaled_for(block):
        part = jnp.dot(rows_of(weight_matrix, block), pool, preferred_element_type=jnp.float32)
        return part, rows_of(local_max, block)

    def merge(first, second):
        (part_a, scale_a), (part_b, scale_b) = first, second
        scale = jnp.maximum(scale_a, scale_b)
        part = part_a * jnp.exp(scale_a - scale)[:, None] + part_b * jnp.exp(scale_b - scale)[:, None]
        return part, scale

    def hop(carried, perm):
        part, scale = carried
        part = lax.ppermute(part.astype(jnp.bfloat16), "slab", perm).astype(jnp.float32)
        return part, lax.ppermute(scale, "slab", perm)

    arrived = []
    if steps_down:
        down = scaled_for(slabs - steps_down)
        for step in range(1, steps_down):
            down = merge(hop(down, ring_down), scaled_for(slabs - steps_down + step))
        arrived.append(hop(down, ring_down))
    if steps_up:
        up = scaled_for(steps_up)
        for step in range(1, steps_up):
            up = merge(hop(up, ring_up), scaled_for(steps_up - step))
        arrived.append(hop(up, ring_up))
    carried = jnp.dot(rows_of(hard_matrix, 0), pool, preferred_element_type=jnp.float32)
    for part, scale in arrived:
        carried = carried + part * jnp.exp(scale - row_lse)[:, None]
    pool_grad = jnp.dot(coef_pool, pool, preferred_element_type=jnp.float32)
    query_grad = pool_grad + carried

    column_queries = jnp.concatenate(query_blocks, axis=0)
    partial = lax.dot_general(
        coef_pool, queries, contract_cols, preferred_element_type=jnp.float32
    ) + lax.dot_general(hard_matrix, column_queries, contract_cols, preferred_element_type=jnp.float32)
    passage_grad = lax.psum_scatter(
        partial.astype(jnp.bfloat16), "blk", scatter_dimension=0, tiled=True
    ).astype(jnp.float32)
    return (query_loss, query_grad, passage_grad)


def solution(mesh):
    return jax.shard_map(
        per_device,
        mesh=mesh,
        in_specs=(
            P(("blk", "slab"), None),
            P(("blk", "slab"), None),
            P(("blk", "slab")),
            P(("blk", "slab"), None),
        ),
        out_specs=(P(("blk", "slab")), P(("blk", "slab"), None), P(("blk", "slab"), None)),
        check_vma=False,
    )
```

```python
import math

import jax
import jax.numpy as jnp
from jax import lax
from jax.sharding import PartitionSpec as P


def per_device(queries, passages, positive, hard_ids):
    slabs = lax.axis_size("slab")
    my_slab = lax.axis_index("slab")
    query_rows_dev, model_width = queries.shape
    passage_rows_dev = passages.shape[0]
    hard_count = hard_ids.shape[1]
    logit_scale = 3.0 / math.sqrt(model_width)
    contract_rows = (((1,), (1,)), ((), ()))
    contract_cols = (((0,), (0,)), ((), ()))

    pool = lax.all_gather(passages, "blk", axis=0, tiled=True)
    pool_size = pool.shape[0]

    ring_down = [(i, (i - 1) % slabs) for i in range(slabs)]
    ring_up = [(i, (i + 1) % slabs) for i in range(slabs)]
    steps_down = slabs // 2
    steps_up = slabs - 1 - steps_down

    def ring_gather(x):
        blocks = [x] * slabs
        current = x
        for step in range(1, steps_down + 1):
            current = lax.ppermute(current, "slab", ring_down)
            blocks[step] = current
        current = x
        for step in range(1, steps_up + 1):
            current = lax.ppermute(current, "slab", ring_up)
            blocks[slabs - step] = current
        return blocks

    query_blocks = ring_gather(queries)
    id_blocks = ring_gather(hard_ids)

    def to_origin(x):
        doubled = jnp.concatenate([x, x], axis=0)
        return lax.dynamic_slice_in_dim(doubled, (slabs - my_slab) % slabs, slabs, axis=0)

    def to_ring(x):
        doubled = jnp.concatenate([x, x], axis=0)
        return lax.dynamic_slice_in_dim(doubled, my_slab, slabs, axis=0)

    scores = jnp.concatenate(
        [
            lax.dot_general(block, pool, contract_rows, preferred_element_type=jnp.float32)
            for block in query_blocks
        ],
        axis=0,
    ) * logit_scale
    column_ids = jnp.concatenate(id_blocks, axis=0)
    column_rows = column_ids.shape[0]
    pooled = scores[:query_rows_dev]

    owner_dev = column_ids // passage_rows_dev
    owner_slab = owner_dev % slabs
    hard_pos = (owner_dev // slabs) * passage_rows_dev + column_ids % passage_rows_dev
    mine = owner_slab == my_slab
    pool_iota = jnp.arange(pool_size, dtype=jnp.int32)[None, None, :]
    hard_hit = (hard_pos[:, :, None] == pool_iota) & mine[:, :, None]
    hard_mine = jnp.sum(jnp.where(hard_hit, scores[:, None, :], 0.0), axis=2)

    pool_max = jnp.max(pooled, axis=1)
    pool_sum = jnp.sum(jnp.exp(pooled - pool_max[:, None]), axis=1)
    hard_origin = to_origin(hard_mine.reshape(slabs, query_rows_dev * hard_count))
    payload = jnp.concatenate([hard_origin.reshape(-1), pool_max, pool_sum])
    far_below = -1e30
    local_max = jnp.max(jnp.where(mine, hard_mine, far_below), axis=1)
    local_max = local_max.astype(jnp.bfloat16).astype(jnp.float32)
    local_weight = jnp.where(mine, jnp.exp(hard_mine - local_max[:, None]), 0.0)
    weight_matrix = jnp.sum(
        jnp.where(hard_hit, local_weight.astype(jnp.bfloat16).astype(jnp.float32)[:, :, None], 0.0),
        axis=1,
    ).astype(jnp.bfloat16)

    def rows_of(x, block):
        return x[block * query_rows_dev : (block + 1) * query_rows_dev]

    def scaled_for(block):
        part = jnp.dot(rows_of(weight_matrix, block), pool, preferred_element_type=jnp.float32)
        return part, rows_of(local_max, block)

    def merge(first, second):
        (part_a, scale_a), (part_b, scale_b) = first, second
        scale = jnp.maximum(scale_a, scale_b)
        part = part_a * jnp.exp(scale_a - scale)[:, None] + part_b * jnp.exp(scale_b - scale)[:, None]
        return part, scale

    def hop(carried, perm):
        part, scale = carried
        scale_row = jnp.zeros((1, model_width), jnp.bfloat16)
        scale_row = lax.dynamic_update_slice(scale_row, scale.astype(jnp.bfloat16)[None], (0, 0))
        sent = lax.ppermute(
            jnp.concatenate([part.astype(jnp.bfloat16), scale_row], axis=0), "slab", perm
        ).astype(jnp.float32)
        return sent[:query_rows_dev], sent[query_rows_dev, :query_rows_dev]

    first_down = scaled_for(slabs - steps_down) if steps_down else None
    first_up = scaled_for(steps_up) if steps_up else None
    (first_down, first_up), payload = lax.optimization_barrier(((first_down, first_up), payload))
    gathered = lax.all_gather(payload, "slab", axis=0)
    hard_split = column_rows * hard_count
    owner_origin = to_origin(owner_slab.reshape(slabs, query_rows_dev * hard_count))
    slab_iota = jnp.arange(slabs, dtype=jnp.int32)[:, None, None]
    hard_all = jnp.sum(
        jnp.where(
            owner_origin[None] == slab_iota,
            gathered[:, :hard_split].reshape(slabs, slabs, query_rows_dev * hard_count),
            0.0,
        ),
        axis=0,
    )
    hard_all = to_ring(hard_all).reshape(column_rows, hard_count)
    stats = to_ring(gathered[:, hard_split:].reshape(slabs, 2, query_rows_dev))
    max_all = stats[:, 0].reshape(column_rows)
    sum_all = stats[:, 1].reshape(column_rows)

    row_top = jnp.maximum(max_all, jnp.max(hard_all, axis=1))
    row_total = sum_all * jnp.exp(max_all - row_top) + jnp.sum(
        jnp.exp(hard_all - row_top[:, None]), axis=1
    )
    lse_all = row_top + jnp.log(row_total)
    row_lse = lse_all[:query_rows_dev]

    onehot = (jnp.arange(pool_size, dtype=jnp.int32)[None, :] == positive[:, None]).astype(
        jnp.float32
    )
    query_loss = row_lse - jnp.sum(onehot * pooled, axis=1)
    coef_pool = (jnp.exp(pooled - row_lse[:, None]) - onehot).astype(jnp.bfloat16)
    coef_hard = jnp.where(
        mine, jnp.exp(hard_mine - lse_all[:, None]).astype(jnp.bfloat16), jnp.zeros((), jnp.bfloat16)
    )
    hard_matrix = jnp.sum(
        jnp.where(hard_hit, coef_hard.astype(jnp.float32)[:, :, None], 0.0), axis=1
    ).astype(jnp.bfloat16)

    arrived = []
    if steps_down:
        down = first_down
        for step in range(1, steps_down):
            down = merge(hop(down, ring_down), scaled_for(slabs - steps_down + step))
        arrived.append(hop(down, ring_down))
    if steps_up:
        up = first_up
        for step in range(1, steps_up):
            up = merge(hop(up, ring_up), scaled_for(steps_up - step))
        arrived.append(hop(up, ring_up))
    carried = jnp.dot(rows_of(hard_matrix, 0), pool, preferred_element_type=jnp.float32)
    for part, scale in arrived:
        carried = carried + part * jnp.exp(scale - row_lse)[:, None]
    pool_grad = jnp.dot(coef_pool, pool, preferred_element_type=jnp.float32)
    query_grad = pool_grad + carried

    column_queries = jnp.concatenate(query_blocks, axis=0)
    partial = lax.dot_general(
        coef_pool, queries, contract_cols, preferred_element_type=jnp.float32
    ) + lax.dot_general(hard_matrix, column_queries, contract_cols, preferred_element_type=jnp.float32)
    passage_grad = lax.psum_scatter(
        partial.astype(jnp.bfloat16), "blk", scatter_dimension=0, tiled=True
    ).astype(jnp.float32)
    return (query_loss, query_grad, passage_grad)


def solution(mesh):
    return jax.shard_map(
        per_device,
        mesh=mesh,
        in_specs=(
            P(("blk", "slab"), None),
            P(("blk", "slab"), None),
            P(("blk", "slab")),
            P(("blk", "slab"), None),
        ),
        out_specs=(P(("blk", "slab")), P(("blk", "slab"), None), P(("blk", "slab"), None)),
        check_vma=False,
    )
```

```python
import math

import jax
import jax.numpy as jnp
from jax import lax
from jax.sharding import PartitionSpec as P


def per_device(queries, passages, positive, hard_ids):
    slabs = lax.axis_size("slab")
    my_slab = lax.axis_index("slab")
    query_rows_dev, model_width = queries.shape
    passage_rows_dev = passages.shape[0]
    hard_count = hard_ids.shape[1]
    logit_scale = 3.0 / math.sqrt(model_width)
    contract_rows = (((1,), (1,)), ((), ()))
    contract_cols = (((0,), (0,)), ((), ()))

    blocks = lax.axis_size("blk")
    pool = lax.all_to_all(
        jnp.broadcast_to(passages[None], (blocks,) + passages.shape), "blk", 0, 0, tiled=True
    ).reshape(blocks * passages.shape[0], passages.shape[1])
    pool_size = pool.shape[0]

    ring_down = [(i, (i - 1) % slabs) for i in range(slabs)]
    ring_up = [(i, (i + 1) % slabs) for i in range(slabs)]
    steps_down = slabs // 2
    steps_up = slabs - 1 - steps_down

    def ring_gather(x):
        blocks = [x] * slabs
        current = x
        for step in range(1, steps_down + 1):
            current = lax.ppermute(current, "slab", ring_down)
            blocks[step] = current
        current = x
        for step in range(1, steps_up + 1):
            current = lax.ppermute(current, "slab", ring_up)
            blocks[slabs - step] = current
        return blocks

    query_blocks = ring_gather(queries)
    id_blocks = ring_gather(hard_ids)

    def to_origin(x):
        doubled = jnp.concatenate([x, x], axis=0)
        return lax.dynamic_slice_in_dim(doubled, (slabs - my_slab) % slabs, slabs, axis=0)

    def to_ring(x):
        doubled = jnp.concatenate([x, x], axis=0)
        return lax.dynamic_slice_in_dim(doubled, my_slab, slabs, axis=0)

    scores = jnp.concatenate(
        [
            lax.dot_general(block, pool, contract_rows, preferred_element_type=jnp.float32)
            for block in query_blocks
        ],
        axis=0,
    ) * logit_scale
    column_ids = jnp.concatenate(id_blocks, axis=0)
    column_rows = column_ids.shape[0]
    pooled = scores[:query_rows_dev]

    owner_dev = column_ids // passage_rows_dev
    owner_slab = owner_dev % slabs
    hard_pos = (owner_dev // slabs) * passage_rows_dev + column_ids % passage_rows_dev
    mine = owner_slab == my_slab
    pool_iota = jnp.arange(pool_size, dtype=jnp.int32)[None, None, :]
    hard_hit = (hard_pos[:, :, None] == pool_iota) & mine[:, :, None]
    hard_mine = jnp.sum(jnp.where(hard_hit, scores[:, None, :], 0.0), axis=2)

    pool_max = jnp.max(pooled, axis=1)
    pool_sum = jnp.sum(jnp.exp(pooled - pool_max[:, None]), axis=1)
    hard_origin = to_origin(hard_mine.reshape(slabs, query_rows_dev * hard_count))
    payload = jnp.concatenate([hard_origin.reshape(-1), pool_max, pool_sum])
    gathered = to_origin(
        jnp.stack(
            [payload]
            + [
                lax.ppermute(payload, "slab", [(i, (i - t) % slabs) for i in range(slabs)])
                for t in range(1, slabs)
            ]
        )
    )
    hard_split = column_rows * hard_count
    owner_origin = to_origin(owner_slab.reshape(slabs, query_rows_dev * hard_count))
    slab_iota = jnp.arange(slabs, dtype=jnp.int32)[:, None, None]
    hard_all = jnp.sum(
        jnp.where(
            owner_origin[None] == slab_iota,
            gathered[:, :hard_split].reshape(slabs, slabs, query_rows_dev * hard_count),
            0.0,
        ),
        axis=0,
    )
    hard_all = to_ring(hard_all).reshape(column_rows, hard_count)
    stats = to_ring(gathered[:, hard_split:].reshape(slabs, 2, query_rows_dev))
    max_all = stats[:, 0].reshape(column_rows)
    sum_all = stats[:, 1].reshape(column_rows)

    row_top = jnp.maximum(max_all, jnp.max(hard_all, axis=1))
    row_total = sum_all * jnp.exp(max_all - row_top) + jnp.sum(
        jnp.exp(hard_all - row_top[:, None]), axis=1
    )
    lse_all = row_top + jnp.log(row_total)
    row_lse = lse_all[:query_rows_dev]

    onehot = (jnp.arange(pool_size, dtype=jnp.int32)[None, :] == positive[:, None]).astype(
        jnp.float32
    )
    query_loss = row_lse - jnp.sum(onehot * pooled, axis=1)
    coef_pool = (jnp.exp(pooled - row_lse[:, None]) - onehot).astype(jnp.bfloat16)
    coef_hard = jnp.where(
        mine, jnp.exp(hard_mine - lse_all[:, None]).astype(jnp.bfloat16), jnp.zeros((), jnp.bfloat16)
    )
    hard_matrix = jnp.sum(
        jnp.where(hard_hit, coef_hard.astype(jnp.float32)[:, :, None], 0.0), axis=1
    ).astype(jnp.bfloat16)

    def grad_for(block):
        rows = hard_matrix[block * query_rows_dev : (block + 1) * query_rows_dev]
        return jnp.dot(rows, pool, preferred_element_type=jnp.float32)

    def hop(part, perm):
        return lax.ppermute(part.astype(jnp.bfloat16), "slab", perm).astype(jnp.float32)

    carried = grad_for(0)
    if steps_down:
        down = grad_for(slabs - steps_down)
        for step in range(1, steps_down):
            down = hop(down, ring_down) + grad_for(slabs - steps_down + step)
        carried = carried + hop(down, ring_down)
    if steps_up:
        up = grad_for(steps_up)
        for step in range(1, steps_up):
            up = hop(up, ring_up) + grad_for(steps_up - step)
        carried = carried + hop(up, ring_up)
    pool_grad = jnp.dot(coef_pool, pool, preferred_element_type=jnp.float32)
    query_grad = pool_grad + carried

    column_queries = jnp.concatenate(query_blocks, axis=0)
    partial = lax.dot_general(
        coef_pool, queries, contract_cols, preferred_element_type=jnp.float32
    ) + lax.dot_general(hard_matrix, column_queries, contract_cols, preferred_element_type=jnp.float32)
    passage_grad = jnp.sum(
        lax.all_to_all(
            partial.astype(jnp.bfloat16).reshape(blocks, passage_rows_dev, model_width),
            "blk",
            0,
            0,
            tiled=True,
        ).astype(jnp.float32),
        axis=0,
    )
    return (query_loss, query_grad, passage_grad)


def solution(mesh):
    return jax.shard_map(
        per_device,
        mesh=mesh,
        in_specs=(
            P(("blk", "slab"), None),
            P(("blk", "slab"), None),
            P(("blk", "slab")),
            P(("blk", "slab"), None),
        ),
        out_specs=(P(("blk", "slab")), P(("blk", "slab"), None), P(("blk", "slab"), None)),
        check_vma=False,
    )
```

```python
import math

import jax
import jax.numpy as jnp
from jax import lax
from jax.sharding import PartitionSpec as P


def per_device(queries, passages, positive, hard_ids):
    slabs = lax.axis_size("slab")
    my_slab = lax.axis_index("slab")
    query_rows_dev, model_width = queries.shape
    passage_rows_dev = passages.shape[0]
    hard_count = hard_ids.shape[1]
    logit_scale = 3.0 / math.sqrt(model_width)
    contract_rows = (((1,), (1,)), ((), ()))
    contract_cols = (((0,), (0,)), ((), ()))

    pool = lax.all_gather(passages, "blk", axis=0, tiled=True)
    pool_size = pool.shape[0]

    ring_down = [(i, (i - 1) % slabs) for i in range(slabs)]
    ring_up = [(i, (i + 1) % slabs) for i in range(slabs)]
    steps_down = slabs // 2
    steps_up = slabs - 1 - steps_down

    def ring_gather(x):
        blocks = [x] * slabs
        current = x
        for step in range(1, steps_down + 1):
            current = lax.ppermute(current, "slab", ring_down)
            blocks[step] = current
        current = x
        for step in range(1, steps_up + 1):
            current = lax.ppermute(current, "slab", ring_up)
            blocks[slabs - step] = current
        return blocks

    query_blocks = ring_gather(queries)
    id_blocks = ring_gather(hard_ids)

    def to_origin(x):
        doubled = jnp.concatenate([x, x], axis=0)
        return lax.dynamic_slice_in_dim(doubled, (slabs - my_slab) % slabs, slabs, axis=0)

    def to_ring(x):
        doubled = jnp.concatenate([x, x], axis=0)
        return lax.dynamic_slice_in_dim(doubled, my_slab, slabs, axis=0)

    score_blocks = [
        lax.dot_general(block, pool, contract_rows, preferred_element_type=jnp.float32) * logit_scale
        for block in query_blocks
    ]
    column_ids = jnp.concatenate(id_blocks, axis=0)
    column_rows = column_ids.shape[0]
    pooled = score_blocks[0]

    owner_dev = column_ids // passage_rows_dev
    owner_slab = owner_dev % slabs
    hard_pos = (owner_dev // slabs) * passage_rows_dev + column_ids % passage_rows_dev
    mine = owner_slab == my_slab
    pool_iota = jnp.arange(pool_size, dtype=jnp.int32)[None, None, :]
    hard_hit = (hard_pos[:, :, None] == pool_iota) & mine[:, :, None]
    hard_mine = jnp.concatenate(
        [
            jnp.sum(
                jnp.where(
                    hard_hit[t * query_rows_dev : (t + 1) * query_rows_dev],
                    block_scores[:, None, :],
                    0.0,
                ),
                axis=2,
            )
            for t, block_scores in enumerate(score_blocks)
        ],
        axis=0,
    )

    pool_max = jnp.max(pooled, axis=1)
    pool_sum = jnp.sum(jnp.exp(pooled - pool_max[:, None]), axis=1)
    hard_origin = to_origin(hard_mine.reshape(slabs, query_rows_dev * hard_count))
    payload = jnp.concatenate([hard_origin.reshape(-1), pool_max, pool_sum])
    gathered = to_origin(
        jnp.stack(
            [payload]
            + [
                lax.ppermute(payload, "slab", [(i, (i - t) % slabs) for i in range(slabs)])
                for t in range(1, slabs)
            ]
        )
    )
    hard_split = column_rows * hard_count
    owner_origin = to_origin(owner_slab.reshape(slabs, query_rows_dev * hard_count))
    slab_iota = jnp.arange(slabs, dtype=jnp.int32)[:, None, None]
    hard_all = jnp.sum(
        jnp.where(
            owner_origin[None] == slab_iota,
            gathered[:, :hard_split].reshape(slabs, slabs, query_rows_dev * hard_count),
            0.0,
        ),
        axis=0,
    )
    hard_all = to_ring(hard_all).reshape(column_rows, hard_count)
    stats = to_ring(gathered[:, hard_split:].reshape(slabs, 2, query_rows_dev))
    max_all = stats[:, 0].reshape(column_rows)
    sum_all = stats[:, 1].reshape(column_rows)

    row_top = jnp.maximum(max_all, jnp.max(hard_all, axis=1))
    row_total = sum_all * jnp.exp(max_all - row_top) + jnp.sum(
        jnp.exp(hard_all - row_top[:, None]), axis=1
    )
    lse_all = row_top + jnp.log(row_total)
    row_lse = lse_all[:query_rows_dev]

    onehot = (jnp.arange(pool_size, dtype=jnp.int32)[None, :] == positive[:, None]).astype(
        jnp.float32
    )
    query_loss = row_lse - jnp.sum(onehot * pooled, axis=1)
    coef_pool = (jnp.exp(pooled - row_lse[:, None]) - onehot).astype(jnp.bfloat16)
    coef_hard = jnp.where(
        mine, jnp.exp(hard_mine - lse_all[:, None]).astype(jnp.bfloat16), jnp.zeros((), jnp.bfloat16)
    )
    hard_matrix = jnp.sum(
        jnp.where(hard_hit, coef_hard.astype(jnp.float32)[:, :, None], 0.0), axis=1
    ).astype(jnp.bfloat16)

    def grad_for(block):
        rows = hard_matrix[block * query_rows_dev : (block + 1) * query_rows_dev]
        return jnp.dot(rows, pool, preferred_element_type=jnp.float32)

    def hop(part, perm):
        return lax.ppermute(part.astype(jnp.bfloat16), "slab", perm).astype(jnp.float32)

    carried = grad_for(0)
    if steps_down:
        down = grad_for(slabs - steps_down)
        for step in range(1, steps_down):
            down = hop(down, ring_down) + grad_for(slabs - steps_down + step)
        carried = carried + hop(down, ring_down)
    if steps_up:
        up = grad_for(steps_up)
        for step in range(1, steps_up):
            up = hop(up, ring_up) + grad_for(steps_up - step)
        carried = carried + hop(up, ring_up)
    pool_grad = jnp.dot(coef_pool, pool, preferred_element_type=jnp.float32)
    query_grad = pool_grad + carried

    column_queries = jnp.concatenate(query_blocks, axis=0)
    partial = lax.dot_general(
        coef_pool, queries, contract_cols, preferred_element_type=jnp.float32
    ) + lax.dot_general(hard_matrix, column_queries, contract_cols, preferred_element_type=jnp.float32)
    passage_grad = lax.psum_scatter(
        partial.astype(jnp.bfloat16), "blk", scatter_dimension=0, tiled=True
    ).astype(jnp.float32)
    return (query_loss, query_grad, passage_grad)


def solution(mesh):
    return jax.shard_map(
        per_device,
        mesh=mesh,
        in_specs=(
            P(("blk", "slab"), None),
            P(("blk", "slab"), None),
            P(("blk", "slab")),
            P(("blk", "slab"), None),
        ),
        out_specs=(P(("blk", "slab")), P(("blk", "slab"), None), P(("blk", "slab"), None)),
        check_vma=False,
    )
```

```python
import math

import jax
import jax.numpy as jnp
from jax import lax
from jax.sharding import PartitionSpec as P


def per_device(queries, passages, positive, hard_ids):
    slabs = lax.axis_size("slab")
    my_slab = lax.axis_index("slab")
    query_rows_dev, model_width = queries.shape
    passage_rows_dev = passages.shape[0]
    hard_count = hard_ids.shape[1]
    logit_scale = 3.0 / math.sqrt(model_width)
    contract_rows = (((1,), (1,)), ((), ()))
    contract_cols = (((0,), (0,)), ((), ()))

    pool = lax.all_gather(passages, "blk", axis=0, tiled=True)
    pool_size = pool.shape[0]

    ring_down = [(i, (i - 1) % slabs) for i in range(slabs)]
    ring_up = [(i, (i + 1) % slabs) for i in range(slabs)]
    steps_down = slabs // 2
    steps_up = slabs - 1 - steps_down

    def ring_gather(x):
        blocks = [x] * slabs
        current = x
        for step in range(1, steps_down + 1):
            current = lax.ppermute(current, "slab", ring_down)
            blocks[step] = current
        current = x
        for step in range(1, steps_up + 1):
            current = lax.ppermute(current, "slab", ring_up)
            blocks[slabs - step] = current
        return blocks

    query_blocks = ring_gather(queries)
    id_blocks = ring_gather(hard_ids)

    def to_origin(x):
        doubled = jnp.concatenate([x, x], axis=0)
        return lax.dynamic_slice_in_dim(doubled, (slabs - my_slab) % slabs, slabs, axis=0)

    def to_ring(x):
        doubled = jnp.concatenate([x, x], axis=0)
        return lax.dynamic_slice_in_dim(doubled, my_slab, slabs, axis=0)

    scores = jnp.concatenate(
        [
            lax.dot_general(block, pool, contract_rows, preferred_element_type=jnp.float32)
            for block in query_blocks
        ],
        axis=0,
    ) * logit_scale
    column_ids = jnp.concatenate(id_blocks, axis=0)
    column_rows = column_ids.shape[0]
    pooled = scores[:query_rows_dev]

    owner_dev = column_ids // passage_rows_dev
    owner_slab = owner_dev % slabs
    hard_pos = (owner_dev // slabs) * passage_rows_dev + column_ids % passage_rows_dev
    mine = owner_slab == my_slab
    pool_iota = jnp.arange(pool_size, dtype=jnp.int32)[None, None, :]
    hard_hit = (hard_pos[:, :, None] == pool_iota) & mine[:, :, None]
    hard_mine = jnp.sum(jnp.where(hard_hit, scores[:, None, :], 0.0), axis=2)

    pool_max = jnp.max(pooled, axis=1)
    pool_sum = jnp.sum(jnp.exp(pooled - pool_max[:, None]), axis=1)
    hard_origin = to_origin(hard_mine.reshape(slabs, query_rows_dev * hard_count))
    payload = jnp.concatenate([hard_origin.reshape(-1), pool_max, pool_sum])
    gathered = to_origin(
        jnp.stack(
            [payload]
            + [
                lax.ppermute(payload, "slab", [(i, (i - t) % slabs) for i in range(slabs)])
                for t in range(1, slabs)
            ]
        )
    )
    hard_split = column_rows * hard_count
    owner_origin = to_origin(owner_slab.reshape(slabs, query_rows_dev * hard_count))
    slab_iota = jnp.arange(slabs, dtype=jnp.int32)[:, None, None]
    hard_all = jnp.sum(
        jnp.where(
            owner_origin[None] == slab_iota,
            gathered[:, :hard_split].reshape(slabs, slabs, query_rows_dev * hard_count),
            0.0,
        ),
        axis=0,
    )
    hard_all = to_ring(hard_all).reshape(column_rows, hard_count)
    stats = to_ring(gathered[:, hard_split:].reshape(slabs, 2, query_rows_dev))
    max_all = stats[:, 0].reshape(column_rows)
    sum_all = stats[:, 1].reshape(column_rows)

    row_top = jnp.maximum(max_all, jnp.max(hard_all, axis=1))
    row_total = sum_all * jnp.exp(max_all - row_top) + jnp.sum(
        jnp.exp(hard_all - row_top[:, None]), axis=1
    )
    lse_all = row_top + jnp.log(row_total)
    row_lse = lse_all[:query_rows_dev]

    onehot = (jnp.arange(pool_size, dtype=jnp.int32)[None, :] == positive[:, None]).astype(
        jnp.float32
    )
    query_loss = row_lse - jnp.sum(onehot * pooled, axis=1)
    coef_pool = (jnp.exp(pooled - row_lse[:, None]) - onehot).astype(jnp.bfloat16)
    coef_hard = jnp.where(
        mine, jnp.exp(hard_mine - lse_all[:, None]).astype(jnp.bfloat16), jnp.zeros((), jnp.bfloat16)
    )
    hard_matrix = jnp.sum(
        jnp.where(hard_hit, coef_hard.astype(jnp.float32)[:, :, None], 0.0), axis=1
    ).astype(jnp.bfloat16)

    def grad_for(block):
        rows = hard_matrix[block * query_rows_dev : (block + 1) * query_rows_dev]
        return jnp.dot(rows, pool, preferred_element_type=jnp.float32)

    def hop(part, perm):
        return lax.ppermute(part.astype(jnp.bfloat16), "slab", perm).astype(jnp.float32)

    carried = grad_for(0)
    if steps_down:
        down = grad_for(slabs - steps_down)
        for step in range(1, steps_down):
            down = hop(down, ring_down) + grad_for(slabs - steps_down + step)
        carried = carried + hop(down, ring_down)
    if steps_up:
        up = grad_for(steps_up)
        for step in range(1, steps_up):
            up = hop(up, ring_up) + grad_for(steps_up - step)
        carried = carried + hop(up, ring_up)
    pool_grad = jnp.dot(coef_pool, pool, preferred_element_type=jnp.float32)
    query_grad = pool_grad + carried

    partial = lax.dot_general(
        jnp.concatenate([coef_pool, hard_matrix], axis=0),
        jnp.concatenate([queries] + query_blocks, axis=0),
        contract_cols,
        preferred_element_type=jnp.float32,
    ).astype(jnp.bfloat16)
    passage_grad = lax.psum_scatter(partial, "blk", scatter_dimension=0, tiled=True).astype(
        jnp.float32
    )
    return (query_loss, query_grad, passage_grad)


def solution(mesh):
    return jax.shard_map(
        per_device,
        mesh=mesh,
        in_specs=(
            P(("blk", "slab"), None),
            P(("blk", "slab"), None),
            P(("blk", "slab")),
            P(("blk", "slab"), None),
        ),
        out_specs=(P(("blk", "slab")), P(("blk", "slab"), None), P(("blk", "slab"), None)),
        check_vma=False,
    )
```

```python
import math

import jax
import jax.numpy as jnp
from jax import lax
from jax.sharding import PartitionSpec as P


def per_device(queries, passages, positive, hard_ids):
    slabs = lax.axis_size("slab")
    my_slab = lax.axis_index("slab")
    query_rows_dev, model_width = queries.shape
    passage_rows_dev = passages.shape[0]
    hard_count = hard_ids.shape[1]
    logit_scale = 3.0 / math.sqrt(model_width)
    contract_rows = (((1,), (1,)), ((), ()))
    contract_cols = (((0,), (0,)), ((), ()))

    pool = lax.all_gather(passages, "blk", axis=0, tiled=True)
    pool_size = pool.shape[0]

    ring_down = [(i, (i - 1) % slabs) for i in range(slabs)]
    ring_up = [(i, (i + 1) % slabs) for i in range(slabs)]
    steps_down = slabs // 2
    steps_up = slabs - 1 - steps_down

    def ring_gather(x):
        blocks = [x] * slabs
        current = x
        for step in range(1, steps_down + 1):
            current = lax.ppermute(current, "slab", ring_down)
            blocks[step] = current
        current = x
        for step in range(1, steps_up + 1):
            current = lax.ppermute(current, "slab", ring_up)
            blocks[slabs - step] = current
        return blocks

    query_blocks = ring_gather(queries)
    id_blocks = ring_gather(hard_ids)

    def to_origin(x):
        doubled = jnp.concatenate([x, x], axis=0)
        return lax.dynamic_slice_in_dim(doubled, (slabs - my_slab) % slabs, slabs, axis=0)

    def to_ring(x):
        doubled = jnp.concatenate([x, x], axis=0)
        return lax.dynamic_slice_in_dim(doubled, my_slab, slabs, axis=0)

    scores = jnp.concatenate(
        [
            lax.dot_general(block, pool, contract_rows, preferred_element_type=jnp.float32)
            for block in query_blocks
        ],
        axis=0,
    ) * logit_scale
    column_ids = jnp.concatenate(id_blocks, axis=0)
    column_rows = column_ids.shape[0]
    pooled = scores[:query_rows_dev]

    owner_dev = column_ids // passage_rows_dev
    owner_slab = owner_dev % slabs
    hard_pos = (owner_dev // slabs) * passage_rows_dev + column_ids % passage_rows_dev
    mine = owner_slab == my_slab
    pool_iota = jnp.arange(pool_size, dtype=jnp.int32)[None, None, :]
    hit_count = jnp.sum(
        ((hard_pos[:, :, None] == pool_iota) & mine[:, :, None]).astype(jnp.float32), axis=1
    )
    is_hard = hit_count > 0
    far_below = -1e30
    hard_max = jnp.max(jnp.where(is_hard, scores, far_below), axis=1)
    hard_sum = jnp.sum(
        jnp.where(is_hard, hit_count * jnp.exp(scores - hard_max[:, None]), 0.0), axis=1
    )

    pool_max = jnp.max(pooled, axis=1)
    pool_sum = jnp.sum(jnp.exp(pooled - pool_max[:, None]), axis=1)
    payload = jnp.concatenate(
        [
            to_origin(hard_max.reshape(slabs, query_rows_dev)).reshape(-1),
            to_origin(hard_sum.reshape(slabs, query_rows_dev)).reshape(-1),
            pool_max,
            pool_sum,
        ]
    )
    gathered = to_origin(
        jnp.stack(
            [payload]
            + [
                lax.ppermute(payload, "slab", [(i, (i - t) % slabs) for i in range(slabs)])
                for t in range(1, slabs)
            ]
        )
    )
    split = column_rows
    max_by_owner = gathered[:, :split].reshape(slabs, slabs, query_rows_dev)
    sum_by_owner = gathered[:, split : 2 * split].reshape(slabs, slabs, query_rows_dev)
    max_pool = gathered[:, 2 * split : 2 * split + query_rows_dev]
    sum_pool = gathered[:, 2 * split + query_rows_dev :]

    row_top = jnp.maximum(max_pool, jnp.max(max_by_owner, axis=0))
    row_total = sum_pool * jnp.exp(max_pool - row_top) + jnp.sum(
        sum_by_owner * jnp.exp(max_by_owner - row_top[None]), axis=0
    )
    lse_all = to_ring(row_top + jnp.log(row_total)).reshape(column_rows)
    row_lse = lse_all[:query_rows_dev]

    onehot = (jnp.arange(pool_size, dtype=jnp.int32)[None, :] == positive[:, None]).astype(
        jnp.float32
    )
    query_loss = row_lse - jnp.sum(onehot * pooled, axis=1)
    coef_pool = (jnp.exp(pooled - row_lse[:, None]) - onehot).astype(jnp.bfloat16)
    hard_matrix = jnp.where(
        is_hard, hit_count * jnp.exp(scores - lse_all[:, None]), 0.0
    ).astype(jnp.bfloat16)

    def grad_for(block):
        rows = hard_matrix[block * query_rows_dev : (block + 1) * query_rows_dev]
        return jnp.dot(rows, pool, preferred_element_type=jnp.float32)

    def hop(part, perm):
        return lax.ppermute(part.astype(jnp.bfloat16), "slab", perm).astype(jnp.float32)

    carried = grad_for(0)
    if steps_down:
        down = grad_for(slabs - steps_down)
        for step in range(1, steps_down):
            down = hop(down, ring_down) + grad_for(slabs - steps_down + step)
        carried = carried + hop(down, ring_down)
    if steps_up:
        up = grad_for(steps_up)
        for step in range(1, steps_up):
            up = hop(up, ring_up) + grad_for(steps_up - step)
        carried = carried + hop(up, ring_up)
    pool_grad = jnp.dot(coef_pool, pool, preferred_element_type=jnp.float32)
    query_grad = pool_grad + carried

    column_queries = jnp.concatenate(query_blocks, axis=0)
    partial = lax.dot_general(
        coef_pool, queries, contract_cols, preferred_element_type=jnp.float32
    ) + lax.dot_general(hard_matrix, column_queries, contract_cols, preferred_element_type=jnp.float32)
    passage_grad = lax.psum_scatter(
        partial.astype(jnp.bfloat16), "blk", scatter_dimension=0, tiled=True
    ).astype(jnp.float32)
    return (query_loss, query_grad, passage_grad)


def solution(mesh):
    return jax.shard_map(
        per_device,
        mesh=mesh,
        in_specs=(
            P(("blk", "slab"), None),
            P(("blk", "slab"), None),
            P(("blk", "slab")),
            P(("blk", "slab"), None),
        ),
        out_specs=(P(("blk", "slab")), P(("blk", "slab"), None), P(("blk", "slab"), None)),
        check_vma=False,
    )
```

```python
import math

import jax
import jax.numpy as jnp
from jax import lax
from jax.sharding import PartitionSpec as P


def per_device(queries, passages, positive, hard_ids):
    slabs = lax.axis_size("slab")
    my_slab = lax.axis_index("slab")
    query_rows_dev, model_width = queries.shape
    passage_rows_dev = passages.shape[0]
    hard_count = hard_ids.shape[1]
    logit_scale = 3.0 / math.sqrt(model_width)
    contract_rows = (((1,), (1,)), ((), ()))
    contract_cols = (((0,), (0,)), ((), ()))

    pool = lax.all_gather(passages, "blk", axis=0, tiled=True)
    pool_size = pool.shape[0]

    ring_down = [(i, (i - 1) % slabs) for i in range(slabs)]
    ring_up = [(i, (i + 1) % slabs) for i in range(slabs)]
    steps_down = slabs // 2
    steps_up = slabs - 1 - steps_down

    def ring_gather(x):
        blocks = [x] * slabs
        current = x
        for step in range(1, steps_down + 1):
            current = lax.ppermute(current, "slab", ring_down)
            blocks[step] = current
        current = x
        for step in range(1, steps_up + 1):
            current = lax.ppermute(current, "slab", ring_up)
            blocks[slabs - step] = current
        return blocks

    query_blocks = ring_gather(queries)
    id_blocks = ring_gather(hard_ids)

    def to_origin(x):
        doubled = jnp.concatenate([x, x], axis=0)
        return lax.dynamic_slice_in_dim(doubled, (slabs - my_slab) % slabs, slabs, axis=0)

    def to_ring(x):
        doubled = jnp.concatenate([x, x], axis=0)
        return lax.dynamic_slice_in_dim(doubled, my_slab, slabs, axis=0)

    scores = jnp.concatenate(
        [
            lax.dot_general(block, pool, contract_rows, preferred_element_type=jnp.float32)
            for block in query_blocks
        ],
        axis=0,
    ) * logit_scale
    column_ids = jnp.concatenate(id_blocks, axis=0)
    column_rows = column_ids.shape[0]
    pooled = scores[:query_rows_dev]

    owner_dev = column_ids // passage_rows_dev
    owner_slab = owner_dev % slabs
    hard_pos = (owner_dev // slabs) * passage_rows_dev + column_ids % passage_rows_dev
    mine = owner_slab == my_slab
    pool_iota = jnp.arange(pool_size, dtype=jnp.int32)[None, None, :]
    hit_count = jnp.sum(
        ((hard_pos[:, :, None] == pool_iota) & mine[:, :, None]).astype(jnp.float32), axis=1
    )
    is_hard = hit_count > 0
    far_below = -1e30
    hard_max = jnp.max(jnp.where(is_hard, scores, far_below), axis=1)
    hard_sum = jnp.sum(
        jnp.where(is_hard, hit_count * jnp.exp(scores - hard_max[:, None]), 0.0), axis=1
    )

    pool_max = jnp.max(pooled, axis=1)
    pool_sum = jnp.sum(jnp.exp(pooled - pool_max[:, None]), axis=1)
    payload = jnp.concatenate(
        [
            to_origin(hard_max.reshape(slabs, query_rows_dev)).reshape(-1),
            to_origin(hard_sum.reshape(slabs, query_rows_dev)).reshape(-1),
            pool_max,
            pool_sum,
        ]
    )
    gathered = to_origin(
        jnp.stack(
            [payload]
            + [
                lax.ppermute(payload, "slab", [(i, (i - t) % slabs) for i in range(slabs)])
                for t in range(1, slabs)
            ]
        )
    )
    split = column_rows
    max_by_owner = gathered[:, :split].reshape(slabs, slabs, query_rows_dev)
    sum_by_owner = gathered[:, split : 2 * split].reshape(slabs, slabs, query_rows_dev)
    max_pool = gathered[:, 2 * split : 2 * split + query_rows_dev]
    sum_pool = gathered[:, 2 * split + query_rows_dev :]

    row_top = jnp.maximum(max_pool, jnp.max(max_by_owner, axis=0))
    row_total = sum_pool * jnp.exp(max_pool - row_top) + jnp.sum(
        sum_by_owner * jnp.exp(max_by_owner - row_top[None]), axis=0
    )
    lse_all = to_ring(row_top + jnp.log(row_total)).reshape(column_rows)
    row_lse = lse_all[:query_rows_dev]

    onehot = (jnp.arange(pool_size, dtype=jnp.int32)[None, :] == positive[:, None]).astype(
        jnp.float32
    )
    query_loss = row_lse - jnp.sum(onehot * pooled, axis=1)
    coef_pool = (jnp.exp(pooled - row_lse[:, None]) - onehot).astype(jnp.bfloat16)
    hard_matrix = jnp.where(
        is_hard, hit_count * jnp.exp(scores - lse_all[:, None]), 0.0
    ).astype(jnp.bfloat16)

    def grad_for(block):
        rows = hard_matrix[block * query_rows_dev : (block + 1) * query_rows_dev]
        return jnp.dot(rows, pool, preferred_element_type=jnp.float32)

    def hop(part, perm):
        return lax.ppermute(part.astype(jnp.bfloat16), "slab", perm).astype(jnp.float32)

    carried = grad_for(0)
    if steps_down:
        down = grad_for(slabs - steps_down)
        for step in range(1, steps_down):
            down = hop(down, ring_down) + grad_for(slabs - steps_down + step)
        carried = carried + hop(down, ring_down)
    column_queries = jnp.concatenate(query_blocks, axis=0)
    partial = lax.dot_general(
        coef_pool, queries, contract_cols, preferred_element_type=jnp.float32
    ) + lax.dot_general(hard_matrix, column_queries, contract_cols, preferred_element_type=jnp.float32)
    passage_grad = lax.psum_scatter(
        partial.astype(jnp.bfloat16), "blk", scatter_dimension=0, tiled=True
    ).astype(jnp.float32)
    if steps_up:
        up = grad_for(steps_up)
        for step in range(1, steps_up):
            up = hop(up, ring_up) + grad_for(steps_up - step)
        up = hop(up, ring_up)
        up, passage_grad = lax.optimization_barrier((up, passage_grad))
        carried = carried + up
    pool_grad = jnp.dot(coef_pool, pool, preferred_element_type=jnp.float32)
    query_grad = pool_grad + carried

    return (query_loss, query_grad, passage_grad)


def solution(mesh):
    return jax.shard_map(
        per_device,
        mesh=mesh,
        in_specs=(
            P(("blk", "slab"), None),
            P(("blk", "slab"), None),
            P(("blk", "slab")),
            P(("blk", "slab"), None),
        ),
        out_specs=(P(("blk", "slab")), P(("blk", "slab"), None), P(("blk", "slab"), None)),
        check_vma=False,
    )
```

```python
import math

import jax
import jax.numpy as jnp
from jax import lax
from jax.sharding import PartitionSpec as P


def per_device(queries, passages, positive, hard_ids):
    slabs = lax.axis_size("slab")
    my_slab = lax.axis_index("slab")
    query_rows_dev, model_width = queries.shape
    passage_rows_dev = passages.shape[0]
    hard_count = hard_ids.shape[1]
    logit_scale = 3.0 / math.sqrt(model_width)
    contract_rows = (((1,), (1,)), ((), ()))
    contract_cols = (((0,), (0,)), ((), ()))

    pool = lax.all_gather(passages, "blk", axis=0, tiled=True)
    pool_size = pool.shape[0]

    ring_down = [(i, (i - 1) % slabs) for i in range(slabs)]
    ring_up = [(i, (i + 1) % slabs) for i in range(slabs)]
    steps_down = slabs // 2
    steps_up = slabs - 1 - steps_down

    def ring_gather(x):
        blocks = [x] * slabs
        current = x
        for step in range(1, steps_down + 1):
            current = lax.ppermute(current, "slab", ring_down)
            blocks[step] = current
        current = x
        for step in range(1, steps_up + 1):
            current = lax.ppermute(current, "slab", ring_up)
            blocks[slabs - step] = current
        return blocks

    query_blocks = ring_gather(queries)
    id_blocks = ring_gather(hard_ids)

    def to_origin(x):
        doubled = jnp.concatenate([x, x], axis=0)
        return lax.dynamic_slice_in_dim(doubled, (slabs - my_slab) % slabs, slabs, axis=0)

    def to_ring(x):
        doubled = jnp.concatenate([x, x], axis=0)
        return lax.dynamic_slice_in_dim(doubled, my_slab, slabs, axis=0)

    scores = jnp.concatenate(
        [
            lax.dot_general(block, pool, contract_rows, preferred_element_type=jnp.float32)
            for block in query_blocks
        ],
        axis=0,
    ) * logit_scale
    column_ids = jnp.concatenate(id_blocks, axis=0)
    column_rows = column_ids.shape[0]
    pooled = scores[:query_rows_dev]

    owner_dev = column_ids // passage_rows_dev
    owner_slab = owner_dev % slabs
    hard_pos = (owner_dev // slabs) * passage_rows_dev + column_ids % passage_rows_dev
    mine = owner_slab == my_slab
    pool_iota = jnp.arange(pool_size, dtype=jnp.int32)[None, None, :]
    hit_count = jnp.sum(
        ((hard_pos[:, :, None] == pool_iota) & mine[:, :, None]).astype(jnp.float32), axis=1
    )
    is_hard = hit_count > 0
    far_below = -1e30
    hard_max = jnp.max(jnp.where(is_hard, scores, far_below), axis=1)
    hard_sum = jnp.sum(
        jnp.where(is_hard, hit_count * jnp.exp(scores - hard_max[:, None]), 0.0), axis=1
    )

    pool_max = jnp.max(pooled, axis=1)
    pool_sum = jnp.sum(jnp.exp(pooled - pool_max[:, None]), axis=1)
    payload = jnp.concatenate(
        [
            to_origin(hard_max.reshape(slabs, query_rows_dev)).reshape(-1),
            to_origin(hard_sum.reshape(slabs, query_rows_dev)).reshape(-1),
            pool_max,
            pool_sum,
        ]
    )
    gathered = to_origin(
        jnp.stack(
            [payload]
            + [
                lax.ppermute(payload, "slab", [(i, (i - t) % slabs) for i in range(slabs)])
                for t in range(1, slabs)
            ]
        )
    )
    split = column_rows
    max_by_owner = gathered[:, :split].reshape(slabs, slabs, query_rows_dev)
    sum_by_owner = gathered[:, split : 2 * split].reshape(slabs, slabs, query_rows_dev)
    max_pool = gathered[:, 2 * split : 2 * split + query_rows_dev]
    sum_pool = gathered[:, 2 * split + query_rows_dev :]

    row_top = jnp.maximum(max_pool, jnp.max(max_by_owner, axis=0))
    row_total = sum_pool * jnp.exp(max_pool - row_top) + jnp.sum(
        sum_by_owner * jnp.exp(max_by_owner - row_top[None]), axis=0
    )
    lse_all = to_ring(row_top + jnp.log(row_total)).reshape(column_rows)
    row_lse = lse_all[:query_rows_dev]

    onehot = (jnp.arange(pool_size, dtype=jnp.int32)[None, :] == positive[:, None]).astype(
        jnp.float32
    )
    query_loss = row_lse - jnp.sum(onehot * pooled, axis=1)
    coef_pool = (jnp.exp(pooled - row_lse[:, None]) - onehot).astype(jnp.bfloat16)
    hard_matrix = jnp.where(
        is_hard, hit_count * jnp.exp(scores - lse_all[:, None]), 0.0
    ).astype(jnp.bfloat16)

    def grad_for(block):
        rows = hard_matrix[block * query_rows_dev : (block + 1) * query_rows_dev]
        return jnp.dot(rows, pool, preferred_element_type=jnp.float32)

    def hop(part, perm):
        return lax.ppermute(part.astype(jnp.bfloat16), "slab", perm).astype(jnp.float32)

    own_coef = (
        coef_pool.astype(jnp.float32) + hard_matrix[:query_rows_dev].astype(jnp.float32)
    ).astype(jnp.bfloat16)
    carried = jnp.dot(own_coef, pool, preferred_element_type=jnp.float32)
    if steps_down:
        down = grad_for(slabs - steps_down)
        for step in range(1, steps_down):
            down = hop(down, ring_down) + grad_for(slabs - steps_down + step)
        carried = carried + hop(down, ring_down)
    column_queries = jnp.concatenate(query_blocks, axis=0)
    partial = lax.dot_general(
        jnp.concatenate([own_coef, hard_matrix[query_rows_dev:]], axis=0),
        column_queries,
        contract_cols,
        preferred_element_type=jnp.float32,
    )
    passage_grad = lax.psum_scatter(
        partial.astype(jnp.bfloat16), "blk", scatter_dimension=0, tiled=True
    ).astype(jnp.float32)
    if steps_up:
        up = grad_for(steps_up)
        for step in range(1, steps_up):
            up = hop(up, ring_up) + grad_for(steps_up - step)
        up = hop(up, ring_up)
        up, passage_grad = lax.optimization_barrier((up, passage_grad))
        carried = carried + up
    query_grad = carried

    return (query_loss, query_grad, passage_grad)


def solution(mesh):
    return jax.shard_map(
        per_device,
        mesh=mesh,
        in_specs=(
            P(("blk", "slab"), None),
            P(("blk", "slab"), None),
            P(("blk", "slab")),
            P(("blk", "slab"), None),
        ),
        out_specs=(P(("blk", "slab")), P(("blk", "slab"), None), P(("blk", "slab"), None)),
        check_vma=False,
    )
```

```python
import math

import jax
import jax.numpy as jnp
from jax import lax
from jax.sharding import PartitionSpec as P


def per_device(queries, passages, positive, hard_ids):
    slabs = lax.axis_size("slab")
    my_slab = lax.axis_index("slab")
    query_rows_dev, model_width = queries.shape
    passage_rows_dev = passages.shape[0]
    hard_count = hard_ids.shape[1]
    logit_scale = 3.0 / math.sqrt(model_width)
    contract_rows = (((1,), (1,)), ((), ()))
    contract_cols = (((0,), (0,)), ((), ()))

    pool = lax.all_gather(passages, "blk", axis=0, tiled=True)
    pool_size = pool.shape[0]

    ring_down = [(i, (i - 1) % slabs) for i in range(slabs)]
    ring_up = [(i, (i + 1) % slabs) for i in range(slabs)]
    steps_down = slabs // 2
    steps_up = slabs - 1 - steps_down

    def ring_gather(x):
        blocks = [x] * slabs
        current = x
        for step in range(1, steps_down + 1):
            current = lax.ppermute(current, "slab", ring_down)
            blocks[step] = current
        current = x
        for step in range(1, steps_up + 1):
            current = lax.ppermute(current, "slab", ring_up)
            blocks[slabs - step] = current
        return blocks

    query_blocks = ring_gather(queries)
    id_blocks = ring_gather(hard_ids)

    def to_origin(x):
        doubled = jnp.concatenate([x, x], axis=0)
        return lax.dynamic_slice_in_dim(doubled, (slabs - my_slab) % slabs, slabs, axis=0)

    def to_ring(x):
        doubled = jnp.concatenate([x, x], axis=0)
        return lax.dynamic_slice_in_dim(doubled, my_slab, slabs, axis=0)

    scores = jnp.concatenate(
        [
            lax.dot_general(block, pool, contract_rows, preferred_element_type=jnp.float32)
            for block in query_blocks
        ],
        axis=0,
    ) * logit_scale
    column_ids = jnp.concatenate(id_blocks, axis=0)
    column_rows = column_ids.shape[0]
    pooled = scores[:query_rows_dev]

    owner_dev = column_ids // passage_rows_dev
    owner_slab = owner_dev % slabs
    hard_pos = (owner_dev // slabs) * passage_rows_dev + column_ids % passage_rows_dev
    mine = owner_slab == my_slab
    pool_iota = jnp.arange(pool_size, dtype=jnp.int32)[None, None, :]
    far_below = -1e30
    counts, maxes, sums = [], [], []
    for t in range(slabs):
        rows = slice(t * query_rows_dev, (t + 1) * query_rows_dev)
        block_scores = scores[rows]
        count = jnp.sum(
            ((hard_pos[rows][:, :, None] == pool_iota) & mine[rows][:, :, None]).astype(
                jnp.float32
            ),
            axis=1,
        )
        top = jnp.max(jnp.where(count > 0, block_scores, far_below), axis=1)
        counts.append(count)
        maxes.append(top)
        sums.append(
            jnp.sum(jnp.where(count > 0, count * jnp.exp(block_scores - top[:, None]), 0.0), axis=1)
        )
    hit_count = jnp.concatenate(counts, axis=0)
    is_hard = hit_count > 0
    hard_max = jnp.concatenate(maxes)
    hard_sum = jnp.concatenate(sums)

    pool_max = jnp.max(pooled, axis=1)
    pool_sum = jnp.sum(jnp.exp(pooled - pool_max[:, None]), axis=1)
    payload = jnp.concatenate(
        [
            to_origin(hard_max.reshape(slabs, query_rows_dev)).reshape(-1),
            to_origin(hard_sum.reshape(slabs, query_rows_dev)).reshape(-1),
            pool_max,
            pool_sum,
        ]
    )
    gathered = to_origin(
        jnp.stack(
            [payload]
            + [
                lax.ppermute(payload, "slab", [(i, (i - t) % slabs) for i in range(slabs)])
                for t in range(1, slabs)
            ]
        )
    )
    split = column_rows
    max_by_owner = gathered[:, :split].reshape(slabs, slabs, query_rows_dev)
    sum_by_owner = gathered[:, split : 2 * split].reshape(slabs, slabs, query_rows_dev)
    max_pool = gathered[:, 2 * split : 2 * split + query_rows_dev]
    sum_pool = gathered[:, 2 * split + query_rows_dev :]

    row_top = jnp.maximum(max_pool, jnp.max(max_by_owner, axis=0))
    row_total = sum_pool * jnp.exp(max_pool - row_top) + jnp.sum(
        sum_by_owner * jnp.exp(max_by_owner - row_top[None]), axis=0
    )
    lse_all = to_ring(row_top + jnp.log(row_total)).reshape(column_rows)
    row_lse = lse_all[:query_rows_dev]

    onehot = (jnp.arange(pool_size, dtype=jnp.int32)[None, :] == positive[:, None]).astype(
        jnp.float32
    )
    query_loss = row_lse - jnp.sum(onehot * pooled, axis=1)
    coef_pool = (jnp.exp(pooled - row_lse[:, None]) - onehot).astype(jnp.bfloat16)
    hard_matrix = jnp.where(
        is_hard, hit_count * jnp.exp(scores - lse_all[:, None]), 0.0
    ).astype(jnp.bfloat16)

    def grad_for(block):
        rows = hard_matrix[block * query_rows_dev : (block + 1) * query_rows_dev]
        return jnp.dot(rows, pool, preferred_element_type=jnp.float32)

    def hop(part, perm):
        return lax.ppermute(part.astype(jnp.bfloat16), "slab", perm).astype(jnp.float32)

    own_coef = (
        coef_pool.astype(jnp.float32) + hard_matrix[:query_rows_dev].astype(jnp.float32)
    ).astype(jnp.bfloat16)
    carried = jnp.dot(own_coef, pool, preferred_element_type=jnp.float32)
    if steps_down:
        down = grad_for(slabs - steps_down)
        for step in range(1, steps_down):
            down = hop(down, ring_down) + grad_for(slabs - steps_down + step)
        carried = carried + hop(down, ring_down)
    column_queries = jnp.concatenate(query_blocks, axis=0)
    partial = lax.dot_general(
        jnp.concatenate([own_coef, hard_matrix[query_rows_dev:]], axis=0),
        column_queries,
        contract_cols,
        preferred_element_type=jnp.float32,
    )
    passage_grad = lax.psum_scatter(
        partial.astype(jnp.bfloat16), "blk", scatter_dimension=0, tiled=True
    ).astype(jnp.float32)
    if steps_up:
        up = grad_for(steps_up)
        for step in range(1, steps_up):
            up = hop(up, ring_up) + grad_for(steps_up - step)
        up = hop(up, ring_up)
        up, passage_grad = lax.optimization_barrier((up, passage_grad))
        carried = carried + up
    query_grad = carried

    return (query_loss, query_grad, passage_grad)


def solution(mesh):
    return jax.shard_map(
        per_device,
        mesh=mesh,
        in_specs=(
            P(("blk", "slab"), None),
            P(("blk", "slab"), None),
            P(("blk", "slab")),
            P(("blk", "slab"), None),
        ),
        out_specs=(P(("blk", "slab")), P(("blk", "slab"), None), P(("blk", "slab"), None)),
        check_vma=False,
    )
```

```python
import math

import jax
import jax.numpy as jnp
from jax import lax
from jax.sharding import PartitionSpec as P


def per_device(queries, passages, positive, hard_ids):
    slabs = lax.axis_size("slab")
    my_slab = lax.axis_index("slab")
    query_rows_dev, model_width = queries.shape
    passage_rows_dev = passages.shape[0]
    hard_count = hard_ids.shape[1]
    logit_scale = 3.0 / math.sqrt(model_width)
    contract_rows = (((1,), (1,)), ((), ()))
    contract_cols = (((0,), (0,)), ((), ()))

    pool = lax.all_gather(passages, "blk", axis=0, tiled=True)
    pool_size = pool.shape[0]

    ring_down = [(i, (i - 1) % slabs) for i in range(slabs)]
    ring_up = [(i, (i + 1) % slabs) for i in range(slabs)]
    steps_down = slabs // 2
    steps_up = slabs - 1 - steps_down

    def ring_gather(x, gates=None):
        blocks = [x] * slabs
        current = x
        for step in range(1, steps_down + 1):
            if gates is not None:
                current, _ = lax.optimization_barrier((current, gates[step]))
            current = lax.ppermute(current, "slab", ring_down)
            blocks[step] = current
        current = x
        for step in range(1, steps_up + 1):
            if gates is not None:
                current, _ = lax.optimization_barrier((current, gates[slabs - step]))
            current = lax.ppermute(current, "slab", ring_up)
            blocks[slabs - step] = current
        return blocks

    id_blocks = ring_gather(hard_ids)
    query_blocks = ring_gather(queries, id_blocks)

    def to_origin(x):
        doubled = jnp.concatenate([x, x], axis=0)
        return lax.dynamic_slice_in_dim(doubled, (slabs - my_slab) % slabs, slabs, axis=0)

    def to_ring(x):
        doubled = jnp.concatenate([x, x], axis=0)
        return lax.dynamic_slice_in_dim(doubled, my_slab, slabs, axis=0)

    scores = jnp.concatenate(
        [
            lax.dot_general(block, pool, contract_rows, preferred_element_type=jnp.float32)
            for block in query_blocks
        ],
        axis=0,
    ) * logit_scale
    column_ids = jnp.concatenate(id_blocks, axis=0)
    column_rows = column_ids.shape[0]
    pooled = scores[:query_rows_dev]

    owner_dev = column_ids // passage_rows_dev
    owner_slab = owner_dev % slabs
    hard_pos = (owner_dev // slabs) * passage_rows_dev + column_ids % passage_rows_dev
    mine = owner_slab == my_slab
    pool_iota = jnp.arange(pool_size, dtype=jnp.int32)[None, None, :]
    hit_count = jnp.sum(
        ((hard_pos[:, :, None] == pool_iota) & mine[:, :, None]).astype(jnp.float32), axis=1
    )
    is_hard = hit_count > 0
    far_below = -1e30
    hard_max = jnp.max(jnp.where(is_hard, scores, far_below), axis=1)
    hard_sum = jnp.sum(
        jnp.where(is_hard, hit_count * jnp.exp(scores - hard_max[:, None]), 0.0), axis=1
    )

    pool_max = jnp.max(pooled, axis=1)
    pool_sum = jnp.sum(jnp.exp(pooled - pool_max[:, None]), axis=1)
    payload = jnp.concatenate(
        [
            to_origin(hard_max.reshape(slabs, query_rows_dev)).reshape(-1),
            to_origin(hard_sum.reshape(slabs, query_rows_dev)).reshape(-1),
            pool_max,
            pool_sum,
        ]
    )
    gathered = to_origin(
        jnp.stack(
            [payload]
            + [
                lax.ppermute(payload, "slab", [(i, (i - t) % slabs) for i in range(slabs)])
                for t in range(1, slabs)
            ]
        )
    )
    split = column_rows
    max_by_owner = gathered[:, :split].reshape(slabs, slabs, query_rows_dev)
    sum_by_owner = gathered[:, split : 2 * split].reshape(slabs, slabs, query_rows_dev)
    max_pool = gathered[:, 2 * split : 2 * split + query_rows_dev]
    sum_pool = gathered[:, 2 * split + query_rows_dev :]

    row_top = jnp.maximum(max_pool, jnp.max(max_by_owner, axis=0))
    row_total = sum_pool * jnp.exp(max_pool - row_top) + jnp.sum(
        sum_by_owner * jnp.exp(max_by_owner - row_top[None]), axis=0
    )
    lse_all = to_ring(row_top + jnp.log(row_total)).reshape(column_rows)
    row_lse = lse_all[:query_rows_dev]

    onehot = (jnp.arange(pool_size, dtype=jnp.int32)[None, :] == positive[:, None]).astype(
        jnp.float32
    )
    query_loss = row_lse - jnp.sum(onehot * pooled, axis=1)
    coef_pool = (jnp.exp(pooled - row_lse[:, None]) - onehot).astype(jnp.bfloat16)
    hard_matrix = jnp.where(
        is_hard, hit_count * jnp.exp(scores - lse_all[:, None]), 0.0
    ).astype(jnp.bfloat16)

    def grad_for(block):
        rows = hard_matrix[block * query_rows_dev : (block + 1) * query_rows_dev]
        return jnp.dot(rows, pool, preferred_element_type=jnp.float32)

    def hop(part, perm):
        return lax.ppermute(part.astype(jnp.bfloat16), "slab", perm).astype(jnp.float32)

    own_coef = (
        coef_pool.astype(jnp.float32) + hard_matrix[:query_rows_dev].astype(jnp.float32)
    ).astype(jnp.bfloat16)
    carried = jnp.dot(own_coef, pool, preferred_element_type=jnp.float32)
    if steps_down:
        down = grad_for(slabs - steps_down)
        for step in range(1, steps_down):
            down = hop(down, ring_down) + grad_for(slabs - steps_down + step)
        carried = carried + hop(down, ring_down)
    column_queries = jnp.concatenate(query_blocks, axis=0)
    partial = lax.dot_general(
        jnp.concatenate([own_coef, hard_matrix[query_rows_dev:]], axis=0),
        column_queries,
        contract_cols,
        preferred_element_type=jnp.float32,
    )
    passage_grad = lax.psum_scatter(
        partial.astype(jnp.bfloat16), "blk", scatter_dimension=0, tiled=True
    ).astype(jnp.float32)
    if steps_up:
        up = grad_for(steps_up)
        for step in range(1, steps_up):
            up = hop(up, ring_up) + grad_for(steps_up - step)
        up = hop(up, ring_up)
        up, passage_grad = lax.optimization_barrier((up, passage_grad))
        carried = carried + up
    query_grad = carried

    return (query_loss, query_grad, passage_grad)


def solution(mesh):
    return jax.shard_map(
        per_device,
        mesh=mesh,
        in_specs=(
            P(("blk", "slab"), None),
            P(("blk", "slab"), None),
            P(("blk", "slab")),
            P(("blk", "slab"), None),
        ),
        out_specs=(P(("blk", "slab")), P(("blk", "slab"), None), P(("blk", "slab"), None)),
        check_vma=False,
    )
```

```python
import math

import jax
import jax.numpy as jnp
from jax import lax
from jax.sharding import PartitionSpec as P


def per_device(queries, passages, positive, hard_ids):
    slabs = lax.axis_size("slab")
    my_slab = lax.axis_index("slab")
    query_rows_dev, model_width = queries.shape
    passage_rows_dev = passages.shape[0]
    hard_count = hard_ids.shape[1]
    logit_scale = 3.0 / math.sqrt(model_width)
    contract_rows = (((1,), (1,)), ((), ()))
    contract_cols = (((0,), (0,)), ((), ()))

    pool = lax.all_gather(passages, "blk", axis=0, tiled=True)
    pool_size = pool.shape[0]

    ring_down = [(i, (i - 1) % slabs) for i in range(slabs)]
    ring_up = [(i, (i + 1) % slabs) for i in range(slabs)]
    steps_down = slabs // 2
    steps_up = slabs - 1 - steps_down

    def ring_gather(x):
        blocks = [x] * slabs
        current = x
        for step in range(1, steps_down + 1):
            current = lax.ppermute(current, "slab", ring_down)
            blocks[step] = current
        current = x
        for step in range(1, steps_up + 1):
            current = lax.ppermute(current, "slab", ring_up)
            blocks[slabs - step] = current
        return blocks

    query_blocks = ring_gather(queries)
    id_blocks = ring_gather(hard_ids)

    def to_origin(x):
        doubled = jnp.concatenate([x, x], axis=0)
        return lax.dynamic_slice_in_dim(doubled, (slabs - my_slab) % slabs, slabs, axis=0)

    def to_ring(x):
        doubled = jnp.concatenate([x, x], axis=0)
        return lax.dynamic_slice_in_dim(doubled, my_slab, slabs, axis=0)

    scores = jnp.concatenate(
        [
            lax.dot_general(block, pool, contract_rows, preferred_element_type=jnp.float32)
            for block in query_blocks
        ],
        axis=0,
    ) * logit_scale
    column_ids = jnp.concatenate(id_blocks, axis=0)
    column_rows = column_ids.shape[0]
    pooled = scores[:query_rows_dev]

    owner_dev = column_ids // passage_rows_dev
    owner_slab = owner_dev % slabs
    hard_pos = (owner_dev // slabs) * passage_rows_dev + column_ids % passage_rows_dev
    mine = owner_slab == my_slab
    pool_iota = jnp.arange(pool_size, dtype=jnp.int32)[None, None, :]
    hit_count = jnp.sum(
        ((hard_pos[:, :, None] == pool_iota) & mine[:, :, None]).astype(jnp.float32), axis=1
    )
    is_hard = hit_count > 0
    far_below = -1e30
    hard_max = jnp.max(jnp.where(is_hard, scores, far_below), axis=1)
    hard_sum = jnp.sum(
        jnp.where(is_hard, hit_count * jnp.exp(scores - hard_max[:, None]), 0.0), axis=1
    )

    pool_max = jnp.max(pooled, axis=1)
    pool_sum = jnp.sum(jnp.exp(pooled - pool_max[:, None]), axis=1)
    payload = jnp.concatenate(
        [
            to_origin(hard_max.reshape(slabs, query_rows_dev)).reshape(-1),
            to_origin(hard_sum.reshape(slabs, query_rows_dev)).reshape(-1),
            pool_max,
            pool_sum,
        ]
    )
    gathered = to_origin(
        jnp.stack(
            [payload]
            + [
                lax.ppermute(payload, "slab", [(i, (i - t) % slabs) for i in range(slabs)])
                for t in range(1, slabs)
            ]
        )
    )
    split = column_rows
    max_by_owner = gathered[:, :split].reshape(slabs, slabs, query_rows_dev)
    sum_by_owner = gathered[:, split : 2 * split].reshape(slabs, slabs, query_rows_dev)
    max_pool = gathered[:, 2 * split : 2 * split + query_rows_dev]
    sum_pool = gathered[:, 2 * split + query_rows_dev :]

    row_top = jnp.maximum(max_pool, jnp.max(max_by_owner, axis=0))
    row_total = sum_pool * jnp.exp(max_pool - row_top) + jnp.sum(
        sum_by_owner * jnp.exp(max_by_owner - row_top[None]), axis=0
    )
    lse_all = to_ring(row_top + jnp.log(row_total)).reshape(column_rows)
    row_lse = lse_all[:query_rows_dev]

    onehot = (jnp.arange(pool_size, dtype=jnp.int32)[None, :] == positive[:, None]).astype(
        jnp.float32
    )
    query_loss = row_lse - jnp.sum(onehot * pooled, axis=1)
    coef_pool = (jnp.exp(pooled - row_lse[:, None]) - onehot).astype(jnp.bfloat16)
    hard_matrix = jnp.where(
        is_hard, hit_count * jnp.exp(scores - lse_all[:, None]), 0.0
    ).astype(jnp.bfloat16)

    def grad_for(block):
        rows = hard_matrix[block * query_rows_dev : (block + 1) * query_rows_dev]
        return jnp.dot(rows, pool, preferred_element_type=jnp.float32)

    def hop(part, perm):
        return lax.ppermute(part.astype(jnp.bfloat16), "slab", perm).astype(jnp.float32)

    own_coef = (
        coef_pool.astype(jnp.float32) + hard_matrix[:query_rows_dev].astype(jnp.float32)
    ).astype(jnp.bfloat16)
    carried = jnp.dot(own_coef, pool, preferred_element_type=jnp.float32)
    first_blocks = [slabs - steps_down] if steps_down else []
    first_blocks += [steps_up] if steps_up else []
    first_parts = jnp.dot(
        jnp.concatenate(
            [hard_matrix[b * query_rows_dev : (b + 1) * query_rows_dev] for b in first_blocks],
            axis=0,
        ),
        pool,
        preferred_element_type=jnp.float32,
    )
    first = {
        b: first_parts[k * query_rows_dev : (k + 1) * query_rows_dev]
        for k, b in enumerate(first_blocks)
    }
    if steps_down:
        down = first[slabs - steps_down]
        for step in range(1, steps_down):
            down = hop(down, ring_down) + grad_for(slabs - steps_down + step)
        carried = carried + hop(down, ring_down)
    column_queries = jnp.concatenate(query_blocks, axis=0)
    partial = lax.dot_general(
        jnp.concatenate([own_coef, hard_matrix[query_rows_dev:]], axis=0),
        column_queries,
        contract_cols,
        preferred_element_type=jnp.float32,
    )
    passage_grad = lax.psum_scatter(
        partial.astype(jnp.bfloat16), "blk", scatter_dimension=0, tiled=True
    ).astype(jnp.float32)
    if steps_up:
        up = first[steps_up]
        for step in range(1, steps_up):
            up = hop(up, ring_up) + grad_for(steps_up - step)
        up = hop(up, ring_up)
        up, passage_grad = lax.optimization_barrier((up, passage_grad))
        carried = carried + up
    query_grad = carried

    return (query_loss, query_grad, passage_grad)


def solution(mesh):
    return jax.shard_map(
        per_device,
        mesh=mesh,
        in_specs=(
            P(("blk", "slab"), None),
            P(("blk", "slab"), None),
            P(("blk", "slab")),
            P(("blk", "slab"), None),
        ),
        out_specs=(P(("blk", "slab")), P(("blk", "slab"), None), P(("blk", "slab"), None)),
        check_vma=False,
    )
```

```python
import math

import jax
import jax.numpy as jnp
from jax import lax
from jax.sharding import PartitionSpec as P


def per_device(queries, passages, positive, hard_ids):
    slabs = lax.axis_size("slab")
    my_slab = lax.axis_index("slab")
    query_rows_dev, model_width = queries.shape
    passage_rows_dev = passages.shape[0]
    hard_count = hard_ids.shape[1]
    logit_scale = 3.0 / math.sqrt(model_width)
    contract_rows = (((1,), (1,)), ((), ()))
    contract_cols = (((0,), (0,)), ((), ()))

    pool = lax.all_gather(passages, "blk", axis=0, tiled=True)
    pool_size = pool.shape[0]

    ring_down = [(i, (i - 1) % slabs) for i in range(slabs)]
    ring_up = [(i, (i + 1) % slabs) for i in range(slabs)]
    steps_down = slabs // 2
    steps_up = slabs - 1 - steps_down

    def ring_gather(x, after_first_down=False):
        blocks = [x] * slabs
        current = x
        for step in range(1, steps_down + 1):
            current = lax.ppermute(current, "slab", ring_down)
            blocks[step] = current
        current = x
        if after_first_down and steps_down and steps_up:
            current, _ = lax.optimization_barrier((current, blocks[1]))
        for step in range(1, steps_up + 1):
            current = lax.ppermute(current, "slab", ring_up)
            blocks[slabs - step] = current
        return blocks

    query_blocks = ring_gather(queries, after_first_down=True)
    id_blocks = ring_gather(hard_ids)

    def to_origin(x):
        doubled = jnp.concatenate([x, x], axis=0)
        return lax.dynamic_slice_in_dim(doubled, (slabs - my_slab) % slabs, slabs, axis=0)

    def to_ring(x):
        doubled = jnp.concatenate([x, x], axis=0)
        return lax.dynamic_slice_in_dim(doubled, my_slab, slabs, axis=0)

    scores = jnp.concatenate(
        [
            lax.dot_general(block, pool, contract_rows, preferred_element_type=jnp.float32)
            for block in query_blocks
        ],
        axis=0,
    ) * logit_scale
    column_ids = jnp.concatenate(id_blocks, axis=0)
    column_rows = column_ids.shape[0]
    pooled = scores[:query_rows_dev]

    owner_dev = column_ids // passage_rows_dev
    owner_slab = owner_dev % slabs
    hard_pos = (owner_dev // slabs) * passage_rows_dev + column_ids % passage_rows_dev
    mine = owner_slab == my_slab
    pool_iota = jnp.arange(pool_size, dtype=jnp.int32)[None, None, :]
    hit_count = jnp.sum(
        ((hard_pos[:, :, None] == pool_iota) & mine[:, :, None]).astype(jnp.float32), axis=1
    )
    is_hard = hit_count > 0
    far_below = -1e30
    hard_max = jnp.max(jnp.where(is_hard, scores, far_below), axis=1)
    hard_sum = jnp.sum(
        jnp.where(is_hard, hit_count * jnp.exp(scores - hard_max[:, None]), 0.0), axis=1
    )

    pool_max = jnp.max(pooled, axis=1)
    pool_sum = jnp.sum(jnp.exp(pooled - pool_max[:, None]), axis=1)
    payload = jnp.concatenate(
        [
            to_origin(hard_max.reshape(slabs, query_rows_dev)).reshape(-1),
            to_origin(hard_sum.reshape(slabs, query_rows_dev)).reshape(-1),
            pool_max,
            pool_sum,
        ]
    )
    gathered = to_origin(
        jnp.stack(
            [payload]
            + [
                lax.ppermute(payload, "slab", [(i, (i - t) % slabs) for i in range(slabs)])
                for t in range(1, slabs)
            ]
        )
    )
    split = column_rows
    max_by_owner = gathered[:, :split].reshape(slabs, slabs, query_rows_dev)
    sum_by_owner = gathered[:, split : 2 * split].reshape(slabs, slabs, query_rows_dev)
    max_pool = gathered[:, 2 * split : 2 * split + query_rows_dev]
    sum_pool = gathered[:, 2 * split + query_rows_dev :]

    row_top = jnp.maximum(max_pool, jnp.max(max_by_owner, axis=0))
    row_total = sum_pool * jnp.exp(max_pool - row_top) + jnp.sum(
        sum_by_owner * jnp.exp(max_by_owner - row_top[None]), axis=0
    )
    lse_all = to_ring(row_top + jnp.log(row_total)).reshape(column_rows)
    row_lse = lse_all[:query_rows_dev]

    onehot = (jnp.arange(pool_size, dtype=jnp.int32)[None, :] == positive[:, None]).astype(
        jnp.float32
    )
    query_loss = row_lse - jnp.sum(onehot * pooled, axis=1)
    coef_pool = (jnp.exp(pooled - row_lse[:, None]) - onehot).astype(jnp.bfloat16)
    hard_matrix = jnp.where(
        is_hard, hit_count * jnp.exp(scores - lse_all[:, None]), 0.0
    ).astype(jnp.bfloat16)

    def grad_for(block):
        rows = hard_matrix[block * query_rows_dev : (block + 1) * query_rows_dev]
        return jnp.dot(rows, pool, preferred_element_type=jnp.float32)

    def hop(part, perm):
        return lax.ppermute(part.astype(jnp.bfloat16), "slab", perm).astype(jnp.float32)

    own_coef = (
        coef_pool.astype(jnp.float32) + hard_matrix[:query_rows_dev].astype(jnp.float32)
    ).astype(jnp.bfloat16)
    carried = jnp.dot(own_coef, pool, preferred_element_type=jnp.float32)
    if steps_down:
        down = grad_for(slabs - steps_down)
        for step in range(1, steps_down):
            down = hop(down, ring_down) + grad_for(slabs - steps_down + step)
        carried = carried + hop(down, ring_down)
    column_queries = jnp.concatenate(query_blocks, axis=0)
    partial = lax.dot_general(
        jnp.concatenate([own_coef, hard_matrix[query_rows_dev:]], axis=0),
        column_queries,
        contract_cols,
        preferred_element_type=jnp.float32,
    )
    passage_grad = lax.psum_scatter(
        partial.astype(jnp.bfloat16), "blk", scatter_dimension=0, tiled=True
    ).astype(jnp.float32)
    if steps_up:
        up = grad_for(steps_up)
        for step in range(1, steps_up):
            up = hop(up, ring_up) + grad_for(steps_up - step)
        up = hop(up, ring_up)
        up, passage_grad = lax.optimization_barrier((up, passage_grad))
        carried = carried + up
    query_grad = carried

    return (query_loss, query_grad, passage_grad)


def solution(mesh):
    return jax.shard_map(
        per_device,
        mesh=mesh,
        in_specs=(
            P(("blk", "slab"), None),
            P(("blk", "slab"), None),
            P(("blk", "slab")),
            P(("blk", "slab"), None),
        ),
        out_specs=(P(("blk", "slab")), P(("blk", "slab"), None), P(("blk", "slab"), None)),
        check_vma=False,
    )
```
